512 devices in a mesh: dp: 32 (over y, x), tensor: 16 (over z, core).
Axes of the slice: x: 4, y: 8, z: 8, core: 2. Of those that a mesh axis runs over, the one named last changes fastest.
Arguments:
- patch_rows: bfloat16 [32, 3072, 1792], P('dp', 'tensor'), may hold values from -6 to 6
- send_rows: int32 [32, 16, 32, 6], P('dp', 'tensor'), may hold values from 0 to 192, as said below
- take_rows: int32 [32, 2048], P('dp', 'tensor'), may hold values from 0 to 191, as said below
- segments: int32 [32, 2048], P('dp', 'tensor'), may hold values from 0 to 41, never falling along the last dimension, each value on 1 to 96 neighbouring positions
- norm_gain: float32 [1792], replicated, may hold values from 0.5 to 5
- qkv_weight: bfloat16 [1792, 2688], P('tensor'), may hold values from -0.125 to 0.125
- out_weight: bfloat16 [896, 1792], P('tensor'), may hold values from -0.1875 to 0.1875
- grad_out: bfloat16 [32, 2048, 1792], P('dp', 'tensor'), may hold values from -6 to 6
Outputs:
- layer_out: bfloat16 [32, 2048, 1792], P('dp', 'tensor')
- patch_grad: bfloat16 [32, 3072, 1792], P('dp', 'tensor')
The draws below stay inside these ranges and needn't reach their ends.
Inputs may be any that keep to these rules, and one draw needn't show every extreme that they name: `send_rows`: for each source device (s, t) the entries below 192 are distinct, 128 in all; for each group they fill slots from 0 on, the rest being 192; some device sends 6 rows to some group. `take_rows`: for each g and t the 128 entries are distinct and name exactly the slots s * 6 + c that hold a row (c below the number of rows that device (s, t) sends to group g). `segments`: along each row the ids never fall and each id covers 1 to 96 positions.
All inputs are finite; a program needn't handle non-finite values.
Results may differ from the reference program's by a relative error of at most 0.009.
The reference program's roundings to bfloat16 on the way count: a program that leaves them out, or rounds other values in their place, can miss the bound.
Values may be sent and summed in bfloat16 or wider, within the bound.
No kernel may reach another device: no remote copies, remote signals or barrier semaphores. Data moves between devices by JAX's collectives and lax.ppermute only.
A program may use at most 128 MiB of HBM per device.

```python
import math
import jax
import jax.numpy as jnp
import numpy as np
from jax import lax

D = 1792
HD = 112
HEADS = 8
TOK_DEV = 128
MOST = 96
SRC = 192
CAP = 6
SEQ = 2048
CHARTS = 42
N_DP = 32
N_TENSOR = 16


def shuffled(key, count, length):
    keys_all = jax.random.split(key, count)
    return jax.vmap(lambda sub_key: jax.random.permutation(sub_key, length))(keys_all)


def route_tables(key):
    base = jax.random.fold_in(key, 71)
    key_amp, key_order, key_shift, key_kept, key_place = jax.random.split(base, 5)
    share = TOK_DEV // N_DP
    half_share = share // 2
    amplitude = jax.random.randint(key_amp, (N_TENSOR, N_DP // 2), 0, half_share + 1)
    amplitude = amplitude.at[:, 0].set(half_share)
    pattern = jnp.stack([amplitude, -amplitude], axis=2).reshape(N_TENSOR, N_DP)
    pattern = jnp.take_along_axis(pattern, shuffled(key_order, N_TENSOR, N_DP), axis=1)
    shifts = shuffled(key_shift, N_TENSOR, N_DP)
    source_ids = jnp.arange(N_DP)[:, None, None]
    place = (source_ids + shifts[None, :, :]) % N_DP
    spread_pattern = jnp.broadcast_to(pattern[None], (N_DP, N_TENSOR, N_DP))
    counts = share + jnp.take_along_axis(spread_pattern, place, axis=2)
    kept = shuffled(key_kept, N_DP * N_TENSOR, SRC).reshape(N_DP, N_TENSOR, SRC)[:, :, :TOK_DEV]
    starts = jnp.cumsum(counts, axis=2) - counts
    slot_ids = jnp.arange(CAP)
    positions = starts[..., None] + slot_ids
    live = slot_ids < counts[..., None]
    positions = jnp.clip(positions, 0, TOK_DEV - 1).reshape(N_DP, N_TENSOR, N_DP * CAP)
    chosen = jnp.take_along_axis(kept, positions, axis=2).reshape(N_DP, N_TENSOR, N_DP, CAP)
    send_table = jnp.where(live, chosen, SRC)
    live_in = jnp.transpose(live, (2, 1, 0, 3)).reshape(N_DP, N_TENSOR, N_DP * CAP)
    flat_ids = jnp.arange(N_DP * CAP)
    ranking = jnp.where(live_in, 0, N_DP * CAP) + flat_ids
    ordered = jnp.argsort(ranking, axis=2)[:, :, :TOK_DEV]
    mixing = shuffled(key_place, N_DP * N_TENSOR, TOK_DEV).reshape(N_DP, N_TENSOR, TOK_DEV)
    take_table = jnp.take_along_axis(ordered, mixing, axis=2).reshape(N_DP, N_TENSOR * TOK_DEV)
    return (send_table.astype(jnp.int32), take_table.astype(jnp.int32))


def draw_send_rows(key, part):
    return route_tables(key)[0]


def draw_take_rows(key, part):
    return route_tables(key)[1]


def draw_norm_gain(key, part):
    sub_key = jax.random.fold_in(key, 13)
    return jax.random.uniform(sub_key, (D,), jnp.float32, 0.5, 1.5)


def block_levels(stream_key, extent, pieces, least, largest):
    def one(dim, parts):
        steps = jax.random.uniform(jax.random.fold_in(jax.random.fold_in(stream_key, 6), dim), (parts,), jnp.float32, least / len(pieces), largest / len(pieces))
        return jnp.repeat(jnp.exp(steps), extent[dim] // parts).reshape((-1,) + (1,) * (len(extent) - dim - 1))

    loudness = one(*pieces[0])
    for cut in pieces[1:]:
        loudness = loudness * one(*cut)
    return loudness


def split_up(amount, total, bound, skew):
    portions = [(1 << 20) // math.isqrt(rank ** skew) + 1 for rank in range(2, amount + 1)]
    rest, given = total - bound - (amount - 1), [1] * (amount - 1)
    while rest > 0:
        movable = [i for i in range(amount - 1) if given[i] < bound]
        pool, budget = sum([portions[i] for i in movable]), rest
        for i in movable:
            extra = min(bound - given[i], max(1, budget * portions[i] // pool), rest)
            given[i] = given[i] + extra
            rest = rest - extra
    return np.array([bound] + given)


def uneven_parts(own_key, count, total, most, slope):
    if count == 2:
        one = jax.random.randint(own_key, (), max(1, total - most), min(most, total - 1) + 1)
        return jnp.stack([one, total - one])
    tallies = jnp.asarray(split_up(count, total, most, slope), jnp.int32)
    pairs = (count - 1) // 2
    donor, sink = tallies[1:1 + 2 * pairs:2], tallies[2:2 + 2 * pairs:2]
    room = jnp.minimum(donor - 1, most - sink)
    passed = jax.random.randint(jax.random.fold_in(own_key, 1), (pairs,), 0, 1 << 20) % (room + 1)
    tallies = tallies.at[1:1 + 2 * pairs:2].set(donor - passed).at[2:2 + 2 * pairs:2].set(sink + passed)
    return tallies[jax.random.permutation(jax.random.fold_in(own_key, 2), count)]


def centred(key, shape, spread, bound, shards=(), kind=jnp.bfloat16):
    result = spread * jax.random.normal(key, shape, jnp.float32)
    if shards:
        result = result * block_levels(key, shape, shards, -0.22, 0.18)
    return jnp.clip(result, -bound, bound).astype(kind)


def setup_inputs(seed: int = 0) -> dict:
    streams_of = jax.random.split(jax.random.key(seed), 9)
    patch_rows = centred(streams_of[0], (N_DP, N_TENSOR * SRC, D), 1.0, 6.0, ((0, 32), (1, 16)))
    send_rows = draw_send_rows(jax.random.fold_in(streams_of[8], 71), 0)
    take_rows = draw_take_rows(jax.random.fold_in(streams_of[8], 71), 0)
    segments = jax.vmap(lambda own: jnp.searchsorted(jnp.cumsum(uneven_parts(own, CHARTS, SEQ, MOST, 1)), jnp.arange(SEQ), side="right"))(jax.random.split(streams_of[3], N_DP)).reshape((N_DP, SEQ)).astype(jnp.int32)
    norm_gain = draw_norm_gain(jax.random.fold_in(streams_of[8], 71), 0)
    qkv_weight = centred(streams_of[5], (D, 3 * HEADS * HD), D ** -0.5, 0.125, ((0, 16),))
    out_weight = centred(streams_of[6], (HEADS * HD, D), (HEADS * HD) ** -0.5, 0.1875, ((0, 16),))
    grad_out = centred(streams_of[7], (N_DP, SEQ, D), 1.0, 6.0, ((0, 32), (1, 16)))
    return {"patch_rows": patch_rows, "send_rows": send_rows, "take_rows": take_rows, "segments": segments, "norm_gain": norm_gain, "qkv_weight": qkv_weight, "out_weight": out_weight, "grad_out": grad_out}


def normalize(rows_in, norm_gain):
    values = rows_in.astype(jnp.float32)
    center = values - lax.optimization_barrier(jnp.mean(values, axis=-1, keepdims=True))
    inv_dev = lax.rsqrt(lax.optimization_barrier(jnp.mean(center * center, axis=-1, keepdims=True)) + 1e-06)
    unit_rows = center * inv_dev
    return (values, unit_rows, inv_dev, (unit_rows * norm_gain).astype(jnp.bfloat16))

def attend(queries, keyval, seg_query, seg_key):
    all_heads = HEADS * HD
    score_scale = HD ** (-0.5)
    query_count = queries.shape[0]
    key_count = keyval.shape[0]
    query_heads = queries.astype(jnp.float32).reshape(query_count, HEADS, HD)
    key_heads = keyval[:, :all_heads].astype(jnp.float32).reshape(key_count, HEADS, HD)
    value_heads = keyval[:, all_heads:].astype(jnp.float32).reshape(key_count, HEADS, HD)
    scores = jnp.einsum('qhd,khd->hqk', query_heads, key_heads) * score_scale
    same_chart = seg_query[:, None] == seg_key[None, :]
    scores = jnp.where(same_chart[None], scores, -jnp.inf)
    row_max = lax.optimization_barrier(jnp.max(scores, axis=2, keepdims=True))
    exp_scores = jnp.exp(scores - row_max)
    attn_probs = exp_scores / lax.optimization_barrier(jnp.sum(exp_scores, axis=2, keepdims=True))
    prob_low = attn_probs.astype(jnp.bfloat16)
    attended = jnp.einsum('hqk,khd->qhd', prob_low.astype(jnp.float32), value_heads)
    return (attn_probs, prob_low, attended.astype(jnp.bfloat16).reshape(query_count, all_heads))

def attend_back(queries, keyval, attn_probs, prob_low, grad_att):
    all_heads = HEADS * HD
    score_scale = HD ** (-0.5)
    query_count = queries.shape[0]
    key_count = keyval.shape[0]
    query_heads = queries.astype(jnp.float32).reshape(query_count, HEADS, HD)
    key_heads = keyval[:, :all_heads].astype(jnp.float32).reshape(key_count, HEADS, HD)
    value_heads = keyval[:, all_heads:].astype(jnp.float32).reshape(key_count, HEADS, HD)
    grad_heads = grad_att.astype(jnp.float32).reshape(query_count, HEADS, HD)
    dprobs = jnp.einsum('qhd,khd->hqk', grad_heads, value_heads)
    row_inner = lax.optimization_barrier(jnp.sum(attn_probs * dprobs, axis=2, keepdims=True))
    dscore = (attn_probs * (dprobs - row_inner) * score_scale).astype(jnp.bfloat16).astype(jnp.float32)
    grad_query = jnp.einsum('hqk,khd->qhd', dscore, key_heads).reshape(query_count, all_heads)
    grad_key = jnp.einsum('hqk,qhd->khd', dscore, query_heads).reshape(key_count, all_heads)
    grad_value = jnp.einsum('hqk,qhd->khd', prob_low.astype(jnp.float32), grad_heads).reshape(key_count, all_heads)
    return (grad_query, jnp.concatenate([grad_key, grad_value], axis=1))

def group_layer(packed, seg_row, grad_rows, norm_gain, qkv_weight, out_weight):
    all_heads = HEADS * HD
    seq_len = packed.shape[0]
    blocks = seq_len // TOK_DEV
    values, unit_rows, inv_dev, normed = normalize(packed, norm_gain)
    projected = jnp.dot(normed, qkv_weight, preferred_element_type=jnp.float32).astype(jnp.bfloat16)
    queries = projected[:, :all_heads].reshape(blocks, TOK_DEV, all_heads)
    seg_plus = seg_row + 1
    keyval_pad = jnp.pad(projected[:, all_heads:], ((MOST, MOST), (0, 0)))
    seg_pad = jnp.pad(seg_plus, (MOST, MOST))
    window = (jnp.arange(blocks)[:, None] * TOK_DEV + jnp.arange(TOK_DEV + 2 * MOST)[None, :]).astype(jnp.int32)
    keyval_win = keyval_pad[window]
    seg_win = seg_pad[window]
    seg_query = seg_plus.reshape(blocks, TOK_DEV)
    attn_probs, prob_low, attended = jax.vmap(attend)(queries, keyval_win, seg_query, seg_win)
    att_rows = attended.reshape(seq_len, all_heads)
    layer_out = (values + jnp.dot(att_rows, out_weight, preferred_element_type=jnp.float32)).astype(jnp.bfloat16)
    grad_att = jnp.dot(grad_rows, out_weight.T, preferred_element_type=jnp.float32).astype(jnp.bfloat16)
    grad_query, grad_kv_win = jax.vmap(attend_back)(queries, keyval_win, attn_probs, prob_low, grad_att.reshape(blocks, TOK_DEV, all_heads))
    grad_kv = jnp.zeros(keyval_pad.shape, jnp.float32).at[window].add(grad_kv_win)[MOST:MOST + seq_len]
    grad_proj = jnp.concatenate([grad_query.reshape(seq_len, all_heads), grad_kv], axis=1).astype(jnp.bfloat16)
    grad_normed = jnp.dot(grad_proj, qkv_weight.T, preferred_element_type=jnp.float32)
    scaled = grad_normed * norm_gain
    grad_unit = scaled - lax.optimization_barrier(jnp.mean(scaled, axis=-1, keepdims=True)) - unit_rows * lax.optimization_barrier(jnp.mean(scaled * unit_rows, axis=-1, keepdims=True))
    grad_packed = (grad_rows.astype(jnp.float32) + inv_dev * grad_unit).astype(jnp.bfloat16)
    return (layer_out, grad_packed)

def reference(patch_rows, send_rows, take_rows, segments, norm_gain, qkv_weight, out_weight, grad_out):
    rows_all = N_DP * N_TENSOR * SRC
    flat_src = jnp.concatenate([patch_rows.reshape(rows_all, D), jnp.zeros((1, D), patch_rows.dtype)], axis=0)
    src_ids = jnp.arange(N_DP, dtype=jnp.int32)[:, None, None, None]
    part_ids = jnp.arange(N_TENSOR, dtype=jnp.int32)[None, :, None, None]
    global_ids = jnp.where(send_rows == SRC, rows_all, src_ids * (N_TENSOR * SRC) + part_ids * SRC + send_rows).astype(jnp.int32)
    slot_ids = jnp.transpose(global_ids, (2, 1, 0, 3)).reshape(N_DP, N_TENSOR, N_DP * CAP)
    picked = jnp.take_along_axis(slot_ids, take_rows.reshape(N_DP, N_TENSOR, TOK_DEV), axis=2).reshape(N_DP, SEQ).astype(jnp.int32)
    packed = flat_src[picked]

    def per_group(group_items):
        return group_layer(group_items[0], group_items[1], group_items[2], norm_gain, qkv_weight, out_weight)
    layer_out, grad_packed = lax.map(per_group, (packed, segments, grad_out))
    grad_flat = jnp.zeros((rows_all + 1, D), grad_packed.dtype).at[picked.reshape(-1)].add(grad_packed.reshape(-1, D))
    patch_grad = grad_flat[:rows_all].reshape(N_DP, N_TENSOR * SRC, D)
    return (layer_out, patch_grad)
```

```python
import jax
import jax.numpy as jnp
from jax import lax
from jax.sharding import Mesh, PartitionSpec as P

HD = 112
HEADS = 8
MOST = 96


def extended(block, sides, width):
    for axis, dim in sides:
        count = lax.axis_size(axis)
        forward = [(i, i + 1) for i in range(count - 1)]
        backward = [(target, source) for source, target in forward]
        low = lax.ppermute(
            lax.slice_in_dim(block, block.shape[dim] - width, None, axis=dim), axis, forward
        )
        high = lax.ppermute(lax.slice_in_dim(block, 0, width, axis=dim), axis, backward)
        block = jnp.concatenate([low, block, high], axis=dim)
    return block


TENSOR = ("z", "c")


def gather_rows(block):
    along_z = lax.all_gather(block, "z", axis=0, tiled=False)
    both = lax.all_gather(along_z, "c", axis=1, tiled=False)
    return both.reshape(-1, block.shape[1])


def normalize(rows_in, norm_gain):
    values = rows_in.astype(jnp.float32)
    center = values - jnp.mean(values, axis=-1, keepdims=True)
    inv_dev = lax.rsqrt(jnp.mean(center * center, axis=-1, keepdims=True) + 1e-06)
    unit_rows = center * inv_dev
    return (values, unit_rows, inv_dev, (unit_rows * norm_gain).astype(jnp.bfloat16))


def split_heads(rows_in):
    return rows_in.reshape(rows_in.shape[0], HEADS, HD)


def attend(queries, keyval, seg_query, seg_key):
    all_heads = HEADS * HD
    score_scale = HD ** (-0.5)
    query_heads = split_heads(queries)
    key_heads = split_heads(keyval[:, :all_heads])
    value_heads = split_heads(keyval[:, all_heads:])
    scores = (
        jnp.einsum("qhd,khd->hqk", query_heads, key_heads, preferred_element_type=jnp.float32)
        * score_scale
    )
    same_chart = seg_query[:, None] == seg_key[None, :]
    scores = jnp.where(same_chart[None], scores, -jnp.inf)
    row_max = jnp.max(scores, axis=2, keepdims=True)
    exp_scores = jnp.exp(scores - row_max)
    row_sum = jnp.sum(exp_scores, axis=2, keepdims=True)
    attn_probs = exp_scores / row_sum
    prob_low = attn_probs.astype(jnp.bfloat16)
    attended = jnp.einsum("hqk,khd->qhd", prob_low, value_heads, preferred_element_type=jnp.float32)
    return (
        attn_probs,
        prob_low,
        attended.astype(jnp.bfloat16).reshape(queries.shape[0], all_heads),
        row_max + jnp.log(row_sum),
    )


def local(patch_rows, send_rows, take_rows, segments, norm_gain, qkv_weight, out_weight, grad_out):
    groups = lax.axis_size("dp")
    src_count = patch_rows.shape[1]
    features = patch_rows.shape[2]
    slot_count = send_rows.shape[3]
    own_rows = take_rows.shape[1]
    all_heads = HEADS * HD
    score_scale = HD ** (-0.5)
    patches = patch_rows[0]
    send_flat = send_rows.reshape(groups * slot_count)
    outgoing = jnp.take(patches, send_flat, axis=0, mode="fill", fill_value=0).reshape(
        groups, slot_count, features
    )
    incoming = lax.all_to_all(outgoing, "dp", split_axis=0, concat_axis=0, tiled=True).reshape(
        groups * slot_count, features
    )
    pick_rows = take_rows[0]
    packed = jnp.take(incoming, pick_rows, axis=0)
    full_qkv, full_out = (gather_rows(qkv_weight), gather_rows(out_weight))
    values, unit_rows, inv_dev, normed = normalize(packed, norm_gain)
    projected = jnp.dot(normed, full_qkv, preferred_element_type=jnp.float32).astype(jnp.bfloat16)
    queries = projected[:, :all_heads]
    keyval = projected[:, all_heads:]
    seg_plus = segments[0] + 1
    wide_kv, wide_seg = (
        extended(keyval, ((TENSOR, 0),), MOST),
        extended(seg_plus, ((TENSOR, 0),), MOST),
    )
    attn_probs, prob_low, attended, log_norm = attend(queries, wide_kv, seg_plus, wide_seg)
    layer_out = (values + jnp.dot(attended, full_out, preferred_element_type=jnp.float32)).astype(
        jnp.bfloat16
    )
    grad_rows = grad_out[0]
    grad_att = lax.dot_general(
        grad_rows, full_out, (((1,), (1,)), ((), ())), preferred_element_type=jnp.float32
    ).astype(jnp.bfloat16)
    query_heads = split_heads(queries)
    grad_heads = split_heads(grad_att)
    wide_keys = split_heads(wide_kv[:, :all_heads])
    wide_values = split_heads(wide_kv[:, all_heads:])
    dprobs = jnp.einsum("qhd,khd->hqk", grad_heads, wide_values, preferred_element_type=jnp.float32)
    row_inner = jnp.sum(attn_probs * dprobs, axis=2, keepdims=True)
    dscore = (attn_probs * (dprobs - row_inner) * score_scale).astype(jnp.bfloat16)
    grad_query = jnp.einsum(
        "hqk,khd->qhd", dscore, wide_keys, preferred_element_type=jnp.float32
    ).reshape(own_rows, all_heads)
    window_rows = wide_kv.shape[0]
    grad_key = jnp.einsum("hqk,qhd->khd", dscore, query_heads, preferred_element_type=jnp.float32)
    grad_value = jnp.einsum(
        "hqk,qhd->khd", prob_low, grad_heads, preferred_element_type=jnp.float32
    )
    grad_window = jnp.concatenate(
        [grad_key.reshape(window_rows, all_heads), grad_value.reshape(window_rows, all_heads)],
        axis=1,
    )
    center = grad_window[MOST : MOST + own_rows]
    rim_parts = jnp.concatenate([grad_window[:MOST], grad_window[MOST + own_rows :]], axis=0)
    arrived = extended(rim_parts, ((TENSOR, 0),), MOST)
    center = center.at[:MOST].add(arrived[:MOST])
    center = center.at[own_rows - MOST :].add(arrived[3 * MOST :])
    grad_proj = jnp.concatenate([grad_query, center], axis=1).astype(jnp.bfloat16)
    grad_normed = lax.dot_general(
        grad_proj, full_qkv, (((1,), (1,)), ((), ())), preferred_element_type=jnp.float32
    )
    scaled = grad_normed * norm_gain
    grad_unit = (
        scaled
        - jnp.mean(scaled, axis=-1, keepdims=True)
        - unit_rows * jnp.mean(scaled * unit_rows, axis=-1, keepdims=True)
    )
    grad_packed = (grad_rows.astype(jnp.float32) + inv_dev * grad_unit).astype(jnp.bfloat16)
    back_slots = (
        jnp.zeros((groups * slot_count, features), jnp.bfloat16).at[pick_rows].set(grad_packed)
    )
    back_slots = back_slots.reshape(groups, slot_count, features)
    returned = lax.all_to_all(back_slots, "dp", split_axis=0, concat_axis=0, tiled=True).reshape(
        groups * slot_count, features
    )
    patch_grad = (
        jnp.zeros((src_count + 1, features), jnp.bfloat16).at[send_flat].add(returned)[:src_count]
    )
    return (layer_out[None], patch_grad[None])


def solution(mesh):
    cores = 2
    split = Mesh(
        mesh.devices.reshape(mesh.devices.shape[0], -1, cores), ("dp", "z", "c")
    )
    return jax.shard_map(
        local,
        mesh=split,
        in_specs=(
            P("dp", TENSOR, None),
            P("dp", TENSOR, None, None),
            P("dp", TENSOR),
            P("dp", TENSOR),
            P(),
            P(TENSOR, None),
            P(TENSOR, None),
            P("dp", TENSOR, None),
        ),
        out_specs=(P("dp", TENSOR, None), P("dp", TENSOR, None)),
        check_vma=False,
    )
```

```python
import jax
import jax.numpy as jnp
from jax import lax
from jax.sharding import PartitionSpec as P

HD = 112
HEADS = 8
MOST = 96


def extended(block, sides, width):
    for axis, dim in sides:
        count = lax.axis_size(axis)
        forward = [(i, i + 1) for i in range(count - 1)]
        backward = [(target, source) for source, target in forward]
        low = lax.ppermute(
            lax.slice_in_dim(block, block.shape[dim] - width, None, axis=dim), axis, forward
        )
        high = lax.ppermute(lax.slice_in_dim(block, 0, width, axis=dim), axis, backward)
        block = jnp.concatenate([low, block, high], axis=dim)
    return block


def gather_weights(qkv_weight, out_weight):
    parts = lax.axis_size("tensor")
    qkv_rows, qkv_cols = qkv_weight.shape
    out_rows, out_cols = out_weight.shape
    out_wide = out_weight.reshape(qkv_rows, out_rows * out_cols // qkv_rows)
    both = lax.all_gather(
        jnp.concatenate([qkv_weight, out_wide], axis=1), "tensor", axis=0, tiled=True
    )
    full_qkv = both[:, :qkv_cols]
    full_out = both[:, qkv_cols:].reshape(parts * out_rows, out_cols)
    return full_qkv, full_out


def normalize(rows_in, norm_gain):
    values = rows_in.astype(jnp.float32)
    center = values - jnp.mean(values, axis=-1, keepdims=True)
    inv_dev = lax.rsqrt(jnp.mean(center * center, axis=-1, keepdims=True) + 1e-06)
    unit_rows = center * inv_dev
    return (values, unit_rows, inv_dev, (unit_rows * norm_gain).astype(jnp.bfloat16))


def split_heads(rows_in):
    return rows_in.reshape(rows_in.shape[0], HEADS, HD)


def attend(queries, keyval, seg_query, seg_key):
    all_heads = HEADS * HD
    score_scale = HD ** (-0.5)
    query_heads = split_heads(queries)
    key_heads = split_heads(keyval[:, :all_heads])
    value_heads = split_heads(keyval[:, all_heads:])
    scores = (
        jnp.einsum("qhd,khd->hqk", query_heads, key_heads, preferred_element_type=jnp.float32)
        * score_scale
    )
    same_chart = seg_query[:, None] == seg_key[None, :]
    scores = jnp.where(same_chart[None], scores, -jnp.inf)
    row_max = jnp.max(scores, axis=2, keepdims=True)
    exp_scores = jnp.exp(scores - row_max)
    row_sum = jnp.sum(exp_scores, axis=2, keepdims=True)
    attn_probs = exp_scores / row_sum
    prob_low = attn_probs.astype(jnp.bfloat16)
    attended = jnp.einsum("hqk,khd->qhd", prob_low, value_heads, preferred_element_type=jnp.float32)
    return (
        attn_probs,
        prob_low,
        attended.astype(jnp.bfloat16).reshape(queries.shape[0], all_heads),
        row_max + jnp.log(row_sum),
    )


def local(patch_rows, send_rows, take_rows, segments, norm_gain, qkv_weight, out_weight, grad_out):
    groups = lax.axis_size("dp")
    src_count = patch_rows.shape[1]
    features = patch_rows.shape[2]
    slot_count = send_rows.shape[3]
    own_rows = take_rows.shape[1]
    all_heads = HEADS * HD
    score_scale = HD ** (-0.5)
    patches = patch_rows[0]
    send_flat = send_rows.reshape(groups * slot_count)
    outgoing = jnp.take(patches, send_flat, axis=0, mode="fill", fill_value=0).reshape(
        groups, slot_count, features
    )
    incoming = lax.all_to_all(outgoing, "dp", split_axis=0, concat_axis=0, tiled=True).reshape(
        groups * slot_count, features
    )
    pick_rows = take_rows[0]
    packed = jnp.take(incoming, pick_rows, axis=0)
    full_qkv, full_out = gather_weights(qkv_weight, out_weight)
    values, unit_rows, inv_dev, normed = normalize(packed, norm_gain)
    projected = jnp.dot(normed, full_qkv, preferred_element_type=jnp.float32).astype(jnp.bfloat16)
    queries = projected[:, :all_heads]
    keyval = projected[:, all_heads:]
    seg_plus = segments[0] + 1
    wide_kv, wide_seg = (
        extended(keyval, (("tensor", 0),), MOST),
        extended(seg_plus, (("tensor", 0),), MOST),
    )
    attn_probs, prob_low, attended, log_norm = attend(queries, wide_kv, seg_plus, wide_seg)
    layer_out = (values + jnp.dot(attended, full_out, preferred_element_type=jnp.float32)).astype(
        jnp.bfloat16
    )
    grad_rows = grad_out[0]
    grad_att = lax.dot_general(
        grad_rows, full_out, (((1,), (1,)), ((), ())), preferred_element_type=jnp.float32
    ).astype(jnp.bfloat16)
    query_heads = split_heads(queries)
    grad_heads = split_heads(grad_att)
    wide_keys = split_heads(wide_kv[:, :all_heads])
    wide_values = split_heads(wide_kv[:, all_heads:])
    dprobs = jnp.einsum("qhd,khd->hqk", grad_heads, wide_values, preferred_element_type=jnp.float32)
    row_inner = jnp.sum(attn_probs * dprobs, axis=2, keepdims=True)
    dscore = (attn_probs * (dprobs - row_inner) * score_scale).astype(jnp.bfloat16)
    grad_query = jnp.einsum(
        "hqk,khd->qhd", dscore, wide_keys, preferred_element_type=jnp.float32
    ).reshape(own_rows, all_heads)
    window_rows = wide_kv.shape[0]
    grad_key = jnp.einsum("hqk,qhd->khd", dscore, query_heads, preferred_element_type=jnp.float32)
    grad_value = jnp.einsum(
        "hqk,qhd->khd", prob_low, grad_heads, preferred_element_type=jnp.float32
    )
    grad_window = jnp.concatenate(
        [grad_key.reshape(window_rows, all_heads), grad_value.reshape(window_rows, all_heads)],
        axis=1,
    )
    center = grad_window[MOST : MOST + own_rows]
    rim_parts = jnp.concatenate([grad_window[:MOST], grad_window[MOST + own_rows :]], axis=0)
    arrived = extended(rim_parts, (("tensor", 0),), MOST)
    center = center.at[:MOST].add(arrived[:MOST])
    center = center.at[own_rows - MOST :].add(arrived[3 * MOST :])
    grad_proj = jnp.concatenate([grad_query, center], axis=1).astype(jnp.bfloat16)
    grad_normed = lax.dot_general(
        grad_proj, full_qkv, (((1,), (1,)), ((), ())), preferred_element_type=jnp.float32
    )
    scaled = grad_normed * norm_gain
    grad_unit = (
        scaled
        - jnp.mean(scaled, axis=-1, keepdims=True)
        - unit_rows * jnp.mean(scaled * unit_rows, axis=-1, keepdims=True)
    )
    grad_packed = (grad_rows.astype(jnp.float32) + inv_dev * grad_unit).astype(jnp.bfloat16)
    back_slots = (
        jnp.zeros((groups * slot_count, features), jnp.bfloat16).at[pick_rows].set(grad_packed)
    )
    back_slots = back_slots.reshape(groups, slot_count, features)
    returned = lax.all_to_all(back_slots, "dp", split_axis=0, concat_axis=0, tiled=True).reshape(
        groups * slot_count, features
    )
    patch_grad = (
        jnp.zeros((src_count + 1, features), jnp.bfloat16).at[send_flat].add(returned)[:src_count]
    )
    return (layer_out[None], patch_grad[None])


def solution(mesh):
    return jax.shard_map(
        local,
        mesh=mesh,
        in_specs=(
            P("dp", "tensor", None),
            P("dp", "tensor", None, None),
            P("dp", "tensor"),
            P("dp", "tensor"),
            P(),
            P("tensor", None),
            P("tensor", None),
            P("dp", "tensor", None),
        ),
        out_specs=(P("dp", "tensor", None), P("dp", "tensor", None)),
        check_vma=False,
    )
```

```python
import jax
import jax.numpy as jnp
from jax import lax
from jax.sharding import PartitionSpec as P

HD = 112
HEADS = 8
MOST = 96


def extended(block, sides, width):
    for axis, dim in sides:
        count = lax.axis_size(axis)
        forward = [(i, i + 1) for i in range(count - 1)]
        backward = [(target, source) for source, target in forward]
        low = lax.ppermute(
            lax.slice_in_dim(block, block.shape[dim] - width, None, axis=dim), axis, forward
        )
        high = lax.ppermute(lax.slice_in_dim(block, 0, width, axis=dim), axis, backward)
        block = jnp.concatenate([low, block, high], axis=dim)
    return block


def gather_weights(qkv_weight, out_weight):
    qkv_rows, qkv_cols = qkv_weight.shape
    out_rows, out_cols = out_weight.shape
    out_wide = out_weight.reshape(qkv_rows, out_rows * out_cols // qkv_rows)
    both = lax.all_gather(
        jnp.concatenate([qkv_weight, out_wide], axis=1), "tensor", axis=0, tiled=True
    )
    full_qkv = both[:, :qkv_cols]
    out_pairs = both[:, qkv_cols:]
    return full_qkv, out_pairs


def spread(cols, side):
    rows = cols.shape[0]
    none = jnp.zeros_like(cols)
    pair = (cols, none) if side == 0 else (none, cols)
    return jnp.stack(pair, axis=-1).reshape(rows, 2 * cols.shape[1])


def times_out(attended, out_pairs):
    halves = [
        jnp.dot(spread(attended, side), out_pairs, preferred_element_type=jnp.float32)
        for side in range(2)
    ]
    return jnp.concatenate(halves, axis=1)


def times_out_t(grad_rows, out_pairs):
    half = out_pairs.shape[1]
    rows = grad_rows.shape[0]
    parts = [
        lax.dot_general(
            grad_rows[:, side * half : (side + 1) * half],
            out_pairs,
            (((1,), (1,)), ((), ())),
            preferred_element_type=jnp.float32,
        ).reshape(rows, -1, 2)[:, :, side]
        for side in range(2)
    ]
    return parts[0] + parts[1]


def normalize(rows_in, norm_gain):
    values = rows_in.astype(jnp.float32)
    center = values - jnp.mean(values, axis=-1, keepdims=True)
    inv_dev = lax.rsqrt(jnp.mean(center * center, axis=-1, keepdims=True) + 1e-06)
    unit_rows = center * inv_dev
    return (values, unit_rows, inv_dev, (unit_rows * norm_gain).astype(jnp.bfloat16))


def split_heads(rows_in):
    return rows_in.reshape(rows_in.shape[0], HEADS, HD)


def attend(queries, keyval, seg_query, seg_key):
    all_heads = HEADS * HD
    score_scale = HD ** (-0.5)
    query_heads = split_heads(queries)
    key_heads = split_heads(keyval[:, :all_heads])
    value_heads = split_heads(keyval[:, all_heads:])
    scores = (
        jnp.einsum("qhd,khd->hqk", query_heads, key_heads, preferred_element_type=jnp.float32)
        * score_scale
    )
    same_chart = seg_query[:, None] == seg_key[None, :]
    scores = jnp.where(same_chart[None], scores, -jnp.inf)
    row_max = jnp.max(scores, axis=2, keepdims=True)
    exp_scores = jnp.exp(scores - row_max)
    row_sum = jnp.sum(exp_scores, axis=2, keepdims=True)
    attn_probs = exp_scores / row_sum
    prob_low = attn_probs.astype(jnp.bfloat16)
    attended = jnp.einsum("hqk,khd->qhd", prob_low, value_heads, preferred_element_type=jnp.float32)
    return (
        attn_probs,
        prob_low,
        attended.astype(jnp.bfloat16).reshape(queries.shape[0], all_heads),
        row_max + jnp.log(row_sum),
    )


def local(patch_rows, send_rows, take_rows, segments, norm_gain, qkv_weight, out_weight, grad_out):
    groups = lax.axis_size("dp")
    src_count = patch_rows.shape[1]
    features = patch_rows.shape[2]
    slot_count = send_rows.shape[3]
    own_rows = take_rows.shape[1]
    all_heads = HEADS * HD
    score_scale = HD ** (-0.5)
    patches = patch_rows[0]
    send_flat = send_rows.reshape(groups * slot_count)
    outgoing = jnp.take(patches, send_flat, axis=0, mode="fill", fill_value=0).reshape(
        groups, slot_count, features
    )
    incoming = lax.all_to_all(outgoing, "dp", split_axis=0, concat_axis=0, tiled=True).reshape(
        groups * slot_count, features
    )
    pick_rows = take_rows[0]
    packed = jnp.take(incoming, pick_rows, axis=0)
    full_qkv, full_out = gather_weights(qkv_weight, out_weight)
    values, unit_rows, inv_dev, normed = normalize(packed, norm_gain)
    projected = jnp.dot(normed, full_qkv, preferred_element_type=jnp.float32).astype(jnp.bfloat16)
    queries = projected[:, :all_heads]
    keyval = projected[:, all_heads:]
    seg_plus = segments[0] + 1
    wide_kv, wide_seg = (
        extended(keyval, (("tensor", 0),), MOST),
        extended(seg_plus, (("tensor", 0),), MOST),
    )
    attn_probs, prob_low, attended, log_norm = attend(queries, wide_kv, seg_plus, wide_seg)
    layer_out = (values + times_out(attended, full_out)).astype(jnp.bfloat16)
    grad_rows = grad_out[0]
    grad_att = times_out_t(grad_rows, full_out).astype(jnp.bfloat16)
    query_heads = split_heads(queries)
    grad_heads = split_heads(grad_att)
    wide_keys = split_heads(wide_kv[:, :all_heads])
    wide_values = split_heads(wide_kv[:, all_heads:])
    dprobs = jnp.einsum("qhd,khd->hqk", grad_heads, wide_values, preferred_element_type=jnp.float32)
    row_inner = jnp.sum(attn_probs * dprobs, axis=2, keepdims=True)
    dscore = (attn_probs * (dprobs - row_inner) * score_scale).astype(jnp.bfloat16)
    grad_query = jnp.einsum(
        "hqk,khd->qhd", dscore, wide_keys, preferred_element_type=jnp.float32
    ).reshape(own_rows, all_heads)
    window_rows = wide_kv.shape[0]
    grad_key = jnp.einsum("hqk,qhd->khd", dscore, query_heads, preferred_element_type=jnp.float32)
    grad_value = jnp.einsum(
        "hqk,qhd->khd", prob_low, grad_heads, preferred_element_type=jnp.float32
    )
    grad_window = jnp.concatenate(
        [grad_key.reshape(window_rows, all_heads), grad_value.reshape(window_rows, all_heads)],
        axis=1,
    )
    center = grad_window[MOST : MOST + own_rows]
    rim_parts = jnp.concatenate([grad_window[:MOST], grad_window[MOST + own_rows :]], axis=0)
    arrived = extended(rim_parts, (("tensor", 0),), MOST)
    center = center.at[:MOST].add(arrived[:MOST])
    center = center.at[own_rows - MOST :].add(arrived[3 * MOST :])
    grad_proj = jnp.concatenate([grad_query, center], axis=1).astype(jnp.bfloat16)
    grad_normed = lax.dot_general(
        grad_proj, full_qkv, (((1,), (1,)), ((), ())), preferred_element_type=jnp.float32
    )
    scaled = grad_normed * norm_gain
    grad_unit = (
        scaled
        - jnp.mean(scaled, axis=-1, keepdims=True)
        - unit_rows * jnp.mean(scaled * unit_rows, axis=-1, keepdims=True)
    )
    grad_packed = (grad_rows.astype(jnp.float32) + inv_dev * grad_unit).astype(jnp.bfloat16)
    back_slots = (
        jnp.zeros((groups * slot_count, features), jnp.bfloat16).at[pick_rows].set(grad_packed)
    )
    back_slots = back_slots.reshape(groups, slot_count, features)
    returned = lax.all_to_all(back_slots, "dp", split_axis=0, concat_axis=0, tiled=True).reshape(
        groups * slot_count, features
    )
    patch_grad = (
        jnp.zeros((src_count + 1, features), jnp.bfloat16).at[send_flat].add(returned)[:src_count]
    )
    return (layer_out[None], patch_grad[None])


def solution(mesh):
    return jax.shard_map(
        local,
        mesh=mesh,
        in_specs=(
            P("dp", "tensor", None),
            P("dp", "tensor", None, None),
            P("dp", "tensor"),
            P("dp", "tensor"),
            P(),
            P("tensor", None),
            P("tensor", None),
            P("dp", "tensor", None),
        ),
        out_specs=(P("dp", "tensor", None), P("dp", "tensor", None)),
        check_vma=False,
    )
```

```python
import jax
import jax.numpy as jnp
from jax import lax
from jax.sharding import PartitionSpec as P

HD = 112
HEADS = 8
MOST = 96


def extended(block, sides, width):
    for axis, dim in sides:
        count = lax.axis_size(axis)
        forward = [(i, i + 1) for i in range(count - 1)]
        backward = [(target, source) for source, target in forward]
        low = lax.ppermute(
            lax.slice_in_dim(block, block.shape[dim] - width, None, axis=dim), axis, forward
        )
        high = lax.ppermute(lax.slice_in_dim(block, 0, width, axis=dim), axis, backward)
        block = jnp.concatenate([low, block, high], axis=dim)
    return block


def gather_weights(qkv_weight, out_weight):
    qkv_rows, qkv_cols = qkv_weight.shape
    out_rows, out_cols = out_weight.shape
    out_wide = out_weight.reshape(qkv_rows, out_rows * out_cols // qkv_rows)
    both = lax.all_gather(
        jnp.concatenate([qkv_weight, out_wide], axis=1), "tensor", axis=0, tiled=True
    )
    full_qkv = both[:, :qkv_cols]
    out_pairs = both[:, qkv_cols:]
    return full_qkv, out_pairs


def spread(cols, side):
    rows = cols.shape[0]
    none = jnp.zeros_like(cols)
    pair = (cols, none) if side == 0 else (none, cols)
    return jnp.stack(pair, axis=-1).reshape(rows, 2 * cols.shape[1])


def times_out(attended, out_pairs):
    halves = [
        jnp.dot(spread(attended, side), out_pairs, preferred_element_type=jnp.float32)
        for side in range(2)
    ]
    return jnp.concatenate(halves, axis=1)


def times_out_t(grad_rows, out_pairs):
    half = out_pairs.shape[1]
    rows = grad_rows.shape[0]
    parts = [
        lax.dot_general(
            grad_rows[:, side * half : (side + 1) * half],
            out_pairs,
            (((1,), (1,)), ((), ())),
            preferred_element_type=jnp.float32,
        ).reshape(rows, -1, 2)[:, :, side]
        for side in range(2)
    ]
    return parts[0] + parts[1]


def normalize(rows_in, norm_gain):
    values = rows_in.astype(jnp.float32)
    center = values - jnp.mean(values, axis=-1, keepdims=True)
    inv_dev = lax.rsqrt(jnp.mean(center * center, axis=-1, keepdims=True) + 1e-06)
    unit_rows = center * inv_dev
    return (values, unit_rows, inv_dev, (unit_rows * norm_gain).astype(jnp.bfloat16))


def head_blocks(rows_in, count):
    tiled = jnp.tile(rows_in, (HEADS, 1))
    row_head = lax.broadcasted_iota(jnp.int32, tiled.shape, 0) // count
    col_head = lax.broadcasted_iota(jnp.int32, tiled.shape, 1) // HD
    return jnp.where(row_head == col_head, tiled, jnp.zeros_like(tiled))


def own_heads(stacked, count):
    row_head = lax.broadcasted_iota(jnp.int32, stacked.shape, 0) // count
    col_head = lax.broadcasted_iota(jnp.int32, stacked.shape, 1) // HD
    kept = jnp.where(row_head == col_head, stacked, jnp.zeros_like(stacked))
    return kept.reshape(HEADS, count, stacked.shape[1]).sum(axis=0)


def rows_dot(a, b):
    return lax.dot_general(a, b, (((1,), (1,)), ((), ())), preferred_element_type=jnp.float32)


def cols_dot(a, b):
    return lax.dot_general(a, b, (((0,), (0,)), ((), ())), preferred_element_type=jnp.float32)


def attend(queries, keyval, seg_query, seg_key):
    all_heads = HEADS * HD
    score_scale = HD ** (-0.5)
    count = queries.shape[0]
    query_blocks = head_blocks(queries, count)
    scores = rows_dot(query_blocks, keyval[:, :all_heads]) * score_scale
    same_chart = jnp.tile(seg_query[:, None] == seg_key[None, :], (HEADS, 1))
    scores = jnp.where(same_chart, scores, -jnp.inf)
    row_max = jnp.max(scores, axis=1, keepdims=True)
    exp_scores = jnp.exp(scores - row_max)
    row_sum = jnp.sum(exp_scores, axis=1, keepdims=True)
    attn_probs = exp_scores / row_sum
    prob_low = attn_probs.astype(jnp.bfloat16)
    mixed = jnp.dot(prob_low, keyval[:, all_heads:], preferred_element_type=jnp.float32)
    attended = own_heads(mixed, count)
    return (attn_probs, prob_low, attended.astype(jnp.bfloat16), query_blocks)


def local(patch_rows, send_rows, take_rows, segments, norm_gain, qkv_weight, out_weight, grad_out):
    groups = lax.axis_size("dp")
    src_count = patch_rows.shape[1]
    features = patch_rows.shape[2]
    slot_count = send_rows.shape[3]
    own_rows = take_rows.shape[1]
    all_heads = HEADS * HD
    score_scale = HD ** (-0.5)
    patches = patch_rows[0]
    send_flat = send_rows.reshape(groups * slot_count)
    outgoing = jnp.take(patches, send_flat, axis=0, mode="fill", fill_value=0).reshape(
        groups, slot_count, features
    )
    incoming = lax.all_to_all(outgoing, "dp", split_axis=0, concat_axis=0, tiled=True).reshape(
        groups * slot_count, features
    )
    pick_rows = take_rows[0]
    packed = jnp.take(incoming, pick_rows, axis=0)
    full_qkv, full_out = gather_weights(qkv_weight, out_weight)
    values, unit_rows, inv_dev, normed = normalize(packed, norm_gain)
    projected = jnp.dot(normed, full_qkv, preferred_element_type=jnp.float32).astype(jnp.bfloat16)
    queries = projected[:, :all_heads]
    keyval = projected[:, all_heads:]
    seg_plus = segments[0] + 1
    wide_kv, wide_seg = (
        extended(keyval, (("tensor", 0),), MOST),
        extended(seg_plus, (("tensor", 0),), MOST),
    )
    attn_probs, prob_low, attended, query_blocks = attend(queries, wide_kv, seg_plus, wide_seg)
    layer_out = (values + times_out(attended, full_out)).astype(jnp.bfloat16)
    grad_rows = grad_out[0]
    grad_att = times_out_t(grad_rows, full_out).astype(jnp.bfloat16)
    grad_blocks = head_blocks(grad_att, own_rows)
    dprobs = rows_dot(grad_blocks, wide_kv[:, all_heads:])
    row_inner = jnp.sum(attn_probs * dprobs, axis=1, keepdims=True)
    dscore = (attn_probs * (dprobs - row_inner) * score_scale).astype(jnp.bfloat16)
    grad_query = own_heads(
        jnp.dot(dscore, wide_kv[:, :all_heads], preferred_element_type=jnp.float32), own_rows
    )
    grad_key = cols_dot(dscore, query_blocks)
    grad_value = cols_dot(prob_low, grad_blocks)
    grad_window = jnp.concatenate([grad_key, grad_value], axis=1)
    center = grad_window[MOST : MOST + own_rows]
    rim_parts = jnp.concatenate([grad_window[:MOST], grad_window[MOST + own_rows :]], axis=0)
    arrived = extended(rim_parts, (("tensor", 0),), MOST)
    center = center.at[:MOST].add(arrived[:MOST])
    center = center.at[own_rows - MOST :].add(arrived[3 * MOST :])
    grad_proj = jnp.concatenate([grad_query, center], axis=1).astype(jnp.bfloat16)
    grad_normed = lax.dot_general(
        grad_proj, full_qkv, (((1,), (1,)), ((), ())), preferred_element_type=jnp.float32
    )
    scaled = grad_normed * norm_gain
    grad_unit = (
        scaled
        - jnp.mean(scaled, axis=-1, keepdims=True)
        - unit_rows * jnp.mean(scaled * unit_rows, axis=-1, keepdims=True)
    )
    grad_packed = (grad_rows.astype(jnp.float32) + inv_dev * grad_unit).astype(jnp.bfloat16)
    back_slots = (
        jnp.zeros((groups * slot_count, features), jnp.bfloat16).at[pick_rows].set(grad_packed)
    )
    back_slots = back_slots.reshape(groups, slot_count, features)
    returned = lax.all_to_all(back_slots, "dp", split_axis=0, concat_axis=0, tiled=True).reshape(
        groups * slot_count, features
    )
    patch_grad = (
        jnp.zeros((src_count + 1, features), jnp.bfloat16).at[send_flat].add(returned)[:src_count]
    )
    return (layer_out[None], patch_grad[None])


def solution(mesh):
    return jax.shard_map(
        local,
        mesh=mesh,
        in_specs=(
            P("dp", "tensor", None),
            P("dp", "tensor", None, None),
            P("dp", "tensor"),
            P("dp", "tensor"),
            P(),
            P("tensor", None),
            P("tensor", None),
            P("dp", "tensor", None),
        ),
        out_specs=(P("dp", "tensor", None), P("dp", "tensor", None)),
        check_vma=False,
    )
```

```python
import jax
import jax.numpy as jnp
from jax import lax
from jax.sharding import PartitionSpec as P

HD = 112
HEADS = 8
MOST = 96


def extended(block, sides, width):
    for axis, dim in sides:
        count = lax.axis_size(axis)
        forward = [(i, i + 1) for i in range(count - 1)]
        backward = [(target, source) for source, target in forward]
        low = lax.ppermute(
            lax.slice_in_dim(block, block.shape[dim] - width, None, axis=dim), axis, forward
        )
        high = lax.ppermute(lax.slice_in_dim(block, 0, width, axis=dim), axis, backward)
        block = jnp.concatenate([low, block, high], axis=dim)
    return block


def ring_gather(block, axis_name):
    count = lax.axis_size(axis_name)
    half = count // 2
    ahead = [(i, (i + 1) % count) for i in range(count)]
    behind = [(i, (i - 1) % count) for i in range(count)]
    forward, backward = block, block
    lower, upper = [], []
    for step in range(1, half + 1):
        forward = lax.ppermute(forward, axis_name, ahead)
        lower.append(forward)
        if step < count - half:
            backward = lax.ppermute(backward, axis_name, behind)
            upper.append(backward)
    offset = ((lax.axis_index(axis_name) - half) % count) * block.shape[0]
    return jnp.concatenate(lower[::-1] + [block] + upper, axis=0), offset


def gather_weights(qkv_weight, out_weight):
    full_qkv = lax.all_gather(qkv_weight, "tensor", axis=0, tiled=True)
    return full_qkv, ring_gather(out_weight, "tensor")


def times_out(attended, out_ring):
    rows, offset = out_ring
    return jnp.dot(jnp.roll(attended, -offset, axis=1), rows, preferred_element_type=jnp.float32)


def times_out_t(grad_rows, out_ring):
    rows, offset = out_ring
    turned = lax.dot_general(
        grad_rows, rows, (((1,), (1,)), ((), ())), preferred_element_type=jnp.float32
    )
    return jnp.roll(turned, offset, axis=1)


def normalize(rows_in, norm_gain):
    values = rows_in.astype(jnp.float32)
    center = values - jnp.mean(values, axis=-1, keepdims=True)
    inv_dev = lax.rsqrt(jnp.mean(center * center, axis=-1, keepdims=True) + 1e-06)
    unit_rows = center * inv_dev
    return (values, unit_rows, inv_dev, (unit_rows * norm_gain).astype(jnp.bfloat16))


def head_blocks(rows_in, count):
    tiled = jnp.tile(rows_in, (HEADS, 1))
    row_head = lax.broadcasted_iota(jnp.int32, tiled.shape, 0) // count
    col_head = lax.broadcasted_iota(jnp.int32, tiled.shape, 1) // HD
    return jnp.where(row_head == col_head, tiled, jnp.zeros_like(tiled))


def own_heads(stacked, count):
    row_head = lax.broadcasted_iota(jnp.int32, stacked.shape, 0) // count
    col_head = lax.broadcasted_iota(jnp.int32, stacked.shape, 1) // HD
    kept = jnp.where(row_head == col_head, stacked, jnp.zeros_like(stacked))
    return kept.reshape(HEADS, count, stacked.shape[1]).sum(axis=0)


def rows_dot(a, b):
    return lax.dot_general(a, b, (((1,), (1,)), ((), ())), preferred_element_type=jnp.float32)


def cols_dot(a, b):
    return lax.dot_general(a, b, (((0,), (0,)), ((), ())), preferred_element_type=jnp.float32)


def attend(queries, keyval, seg_query, seg_key):
    all_heads = HEADS * HD
    score_scale = HD ** (-0.5)
    count = queries.shape[0]
    query_blocks = head_blocks(queries, count)
    scores = rows_dot(query_blocks, keyval[:, :all_heads]) * score_scale
    same_chart = jnp.tile(seg_query[:, None] == seg_key[None, :], (HEADS, 1))
    scores = jnp.where(same_chart, scores, -jnp.inf)
    row_max = jnp.max(scores, axis=1, keepdims=True)
    exp_scores = jnp.exp(scores - row_max)
    row_sum = jnp.sum(exp_scores, axis=1, keepdims=True)
    attn_probs = exp_scores / row_sum
    prob_low = attn_probs.astype(jnp.bfloat16)
    mixed = jnp.dot(prob_low, keyval[:, all_heads:], preferred_element_type=jnp.float32)
    attended = own_heads(mixed, count)
    return (attn_probs, prob_low, attended.astype(jnp.bfloat16), query_blocks)


def local(patch_rows, send_rows, take_rows, segments, norm_gain, qkv_weight, out_weight, grad_out):
    groups = lax.axis_size("dp")
    src_count = patch_rows.shape[1]
    features = patch_rows.shape[2]
    slot_count = send_rows.shape[3]
    own_rows = take_rows.shape[1]
    all_heads = HEADS * HD
    score_scale = HD ** (-0.5)
    patches = patch_rows[0]
    send_flat = send_rows.reshape(groups * slot_count)
    outgoing = jnp.take(patches, send_flat, axis=0, mode="fill", fill_value=0).reshape(
        groups, slot_count, features
    )
    incoming = lax.all_to_all(outgoing, "dp", split_axis=0, concat_axis=0, tiled=True).reshape(
        groups * slot_count, features
    )
    pick_rows = take_rows[0]
    packed = jnp.take(incoming, pick_rows, axis=0)
    full_qkv, full_out = gather_weights(qkv_weight, out_weight)
    values, unit_rows, inv_dev, normed = normalize(packed, norm_gain)
    projected = jnp.dot(normed, full_qkv, preferred_element_type=jnp.float32).astype(jnp.bfloat16)
    queries = projected[:, :all_heads]
    keyval = projected[:, all_heads:]
    seg_plus = segments[0] + 1
    wide_kv, wide_seg = (
        extended(keyval, (("tensor", 0),), MOST),
        extended(seg_plus, (("tensor", 0),), MOST),
    )
    attn_probs, prob_low, attended, query_blocks = attend(queries, wide_kv, seg_plus, wide_seg)
    layer_out = (values + times_out(attended, full_out)).astype(jnp.bfloat16)
    grad_rows = grad_out[0]
    grad_att = times_out_t(grad_rows, full_out).astype(jnp.bfloat16)
    grad_blocks = head_blocks(grad_att, own_rows)
    dprobs = rows_dot(grad_blocks, wide_kv[:, all_heads:])
    row_inner = jnp.sum(attn_probs * dprobs, axis=1, keepdims=True)
    dscore = (attn_probs * (dprobs - row_inner) * score_scale).astype(jnp.bfloat16)
    grad_query = own_heads(
        jnp.dot(dscore, wide_kv[:, :all_heads], preferred_element_type=jnp.float32), own_rows
    )
    grad_key = cols_dot(dscore, query_blocks)
    grad_value = cols_dot(prob_low, grad_blocks)
    grad_window = jnp.concatenate([grad_key, grad_value], axis=1)
    center = grad_window[MOST : MOST + own_rows]
    rim_parts = jnp.concatenate([grad_window[:MOST], grad_window[MOST + own_rows :]], axis=0)
    arrived = extended(rim_parts, (("tensor", 0),), MOST)
    center = center.at[:MOST].add(arrived[:MOST])
    center = center.at[own_rows - MOST :].add(arrived[3 * MOST :])
    grad_proj = jnp.concatenate([grad_query, center], axis=1).astype(jnp.bfloat16)
    grad_normed = lax.dot_general(
        grad_proj, full_qkv, (((1,), (1,)), ((), ())), preferred_element_type=jnp.float32
    )
    scaled = grad_normed * norm_gain
    grad_unit = (
        scaled
        - jnp.mean(scaled, axis=-1, keepdims=True)
        - unit_rows * jnp.mean(scaled * unit_rows, axis=-1, keepdims=True)
    )
    grad_packed = (grad_rows.astype(jnp.float32) + inv_dev * grad_unit).astype(jnp.bfloat16)
    back_slots = (
        jnp.zeros((groups * slot_count, features), jnp.bfloat16).at[pick_rows].set(grad_packed)
    )
    back_slots = back_slots.reshape(groups, slot_count, features)
    returned = lax.all_to_all(back_slots, "dp", split_axis=0, concat_axis=0, tiled=True).reshape(
        groups * slot_count, features
    )
    patch_grad = (
        jnp.zeros((src_count + 1, features), jnp.bfloat16).at[send_flat].add(returned)[:src_count]
    )
    return (layer_out[None], patch_grad[None])


def solution(mesh):
    return jax.shard_map(
        local,
        mesh=mesh,
        in_specs=(
            P("dp", "tensor", None),
            P("dp", "tensor", None, None),
            P("dp", "tensor"),
            P("dp", "tensor"),
            P(),
            P("tensor", None),
            P("tensor", None),
            P("dp", "tensor", None),
        ),
        out_specs=(P("dp", "tensor", None), P("dp", "tensor", None)),
        check_vma=False,
    )
```

```python
import jax
import jax.numpy as jnp
from jax import lax
from jax.sharding import Mesh, PartitionSpec as P

HD = 112
HEADS = 8
MOST = 96


def extended(block, sides, width):
    for axis, dim in sides:
        count = lax.axis_size(axis)
        forward = [(i, i + 1) for i in range(count - 1)]
        backward = [(target, source) for source, target in forward]
        low = lax.ppermute(
            lax.slice_in_dim(block, block.shape[dim] - width, None, axis=dim), axis, forward
        )
        high = lax.ppermute(lax.slice_in_dim(block, 0, width, axis=dim), axis, backward)
        block = jnp.concatenate([low, block, high], axis=dim)
    return block


DP = ("dh", "dl")


def gather_weights(qkv_weight, out_weight):
    qkv_rows, qkv_cols = qkv_weight.shape
    out_rows, out_cols = out_weight.shape
    out_wide = out_weight.reshape(qkv_rows, out_rows * out_cols // qkv_rows)
    both = jnp.concatenate([qkv_weight, out_wide], axis=1)
    half = both.shape[1] // 2
    mine = lax.dynamic_slice_in_dim(both, lax.axis_index("dl") * half, half, axis=1)
    got = lax.all_gather(mine, ("dl", "tensor"), axis=0, tiled=False)
    sides = got.reshape(2, -1, half)
    rest = qkv_cols - half
    return sides[0], sides[1][:, :rest], sides[1][:, rest:]


def spread(cols, side):
    rows = cols.shape[0]
    none = jnp.zeros_like(cols)
    pair = (cols, none) if side == 0 else (none, cols)
    return jnp.stack(pair, axis=-1).reshape(rows, 2 * cols.shape[1])


def times_out(attended, out_pairs):
    halves = [
        jnp.dot(spread(attended, side), out_pairs, preferred_element_type=jnp.float32)
        for side in range(2)
    ]
    return jnp.concatenate(halves, axis=1)


def times_out_t(grad_rows, out_pairs):
    half = out_pairs.shape[1]
    rows = grad_rows.shape[0]
    parts = [
        lax.dot_general(
            grad_rows[:, side * half : (side + 1) * half],
            out_pairs,
            (((1,), (1,)), ((), ())),
            preferred_element_type=jnp.float32,
        ).reshape(rows, -1, 2)[:, :, side]
        for side in range(2)
    ]
    return parts[0] + parts[1]


def normalize(rows_in, norm_gain):
    values = rows_in.astype(jnp.float32)
    center = values - jnp.mean(values, axis=-1, keepdims=True)
    inv_dev = lax.rsqrt(jnp.mean(center * center, axis=-1, keepdims=True) + 1e-06)
    unit_rows = center * inv_dev
    return (values, unit_rows, inv_dev, (unit_rows * norm_gain).astype(jnp.bfloat16))


def head_blocks(rows_in, count):
    tiled = jnp.tile(rows_in, (HEADS, 1))
    row_head = lax.broadcasted_iota(jnp.int32, tiled.shape, 0) // count
    col_head = lax.broadcasted_iota(jnp.int32, tiled.shape, 1) // HD
    return jnp.where(row_head == col_head, tiled, jnp.zeros_like(tiled))


def own_heads(stacked, count):
    row_head = lax.broadcasted_iota(jnp.int32, stacked.shape, 0) // count
    col_head = lax.broadcasted_iota(jnp.int32, stacked.shape, 1) // HD
    kept = jnp.where(row_head == col_head, stacked, jnp.zeros_like(stacked))
    return kept.reshape(HEADS, count, stacked.shape[1]).sum(axis=0)


def rows_dot(a, b):
    return lax.dot_general(a, b, (((1,), (1,)), ((), ())), preferred_element_type=jnp.float32)


def cols_dot(a, b):
    return lax.dot_general(a, b, (((0,), (0,)), ((), ())), preferred_element_type=jnp.float32)


def attend(queries, keyval, seg_query, seg_key):
    all_heads = HEADS * HD
    score_scale = HD ** (-0.5)
    count = queries.shape[0]
    query_blocks = head_blocks(queries, count)
    scores = rows_dot(query_blocks, keyval[:, :all_heads]) * score_scale
    same_chart = jnp.tile(seg_query[:, None] == seg_key[None, :], (HEADS, 1))
    scores = jnp.where(same_chart, scores, -jnp.inf)
    row_max = jnp.max(scores, axis=1, keepdims=True)
    exp_scores = jnp.exp(scores - row_max)
    row_sum = jnp.sum(exp_scores, axis=1, keepdims=True)
    attn_probs = exp_scores / row_sum
    prob_low = attn_probs.astype(jnp.bfloat16)
    mixed = jnp.dot(prob_low, keyval[:, all_heads:], preferred_element_type=jnp.float32)
    attended = own_heads(mixed, count)
    return (attn_probs, prob_low, attended.astype(jnp.bfloat16), query_blocks)


def local(patch_rows, send_rows, take_rows, segments, norm_gain, qkv_weight, out_weight, grad_out):
    groups = lax.axis_size(DP)
    src_count = patch_rows.shape[1]
    features = patch_rows.shape[2]
    slot_count = send_rows.shape[3]
    own_rows = take_rows.shape[1]
    all_heads = HEADS * HD
    score_scale = HD ** (-0.5)
    patches = patch_rows[0]
    send_flat = send_rows.reshape(groups * slot_count)
    outgoing = jnp.take(patches, send_flat, axis=0, mode="fill", fill_value=0).reshape(
        groups, slot_count, features
    )
    incoming = lax.all_to_all(outgoing, DP, split_axis=0, concat_axis=0, tiled=True).reshape(
        groups * slot_count, features
    )
    pick_rows = take_rows[0]
    packed = jnp.take(incoming, pick_rows, axis=0)
    qkv_low, qkv_high, full_out = gather_weights(qkv_weight, out_weight)
    values, unit_rows, inv_dev, normed = normalize(packed, norm_gain)
    proj_low = jnp.dot(normed, qkv_low, preferred_element_type=jnp.float32).astype(jnp.bfloat16)
    proj_high = jnp.dot(normed, qkv_high, preferred_element_type=jnp.float32).astype(jnp.bfloat16)
    queries = proj_low[:, :all_heads]
    keyval = jnp.concatenate([proj_low[:, all_heads:], proj_high], axis=1)
    seg_plus = segments[0] + 1
    wide_kv, wide_seg = (
        extended(keyval, (("tensor", 0),), MOST),
        extended(seg_plus, (("tensor", 0),), MOST),
    )
    attn_probs, prob_low, attended, query_blocks = attend(queries, wide_kv, seg_plus, wide_seg)
    layer_out = (values + times_out(attended, full_out)).astype(jnp.bfloat16)
    grad_rows = grad_out[0]
    grad_att = times_out_t(grad_rows, full_out).astype(jnp.bfloat16)
    grad_blocks = head_blocks(grad_att, own_rows)
    dprobs = rows_dot(grad_blocks, wide_kv[:, all_heads:])
    row_inner = jnp.sum(attn_probs * dprobs, axis=1, keepdims=True)
    dscore = (attn_probs * (dprobs - row_inner) * score_scale).astype(jnp.bfloat16)
    grad_query = own_heads(
        jnp.dot(dscore, wide_kv[:, :all_heads], preferred_element_type=jnp.float32), own_rows
    )
    grad_key = cols_dot(dscore, query_blocks)
    grad_value = cols_dot(prob_low, grad_blocks)
    grad_window = jnp.concatenate([grad_key, grad_value], axis=1)
    center = grad_window[MOST : MOST + own_rows]
    rim_parts = jnp.concatenate([grad_window[:MOST], grad_window[MOST + own_rows :]], axis=0)
    arrived = extended(rim_parts, (("tensor", 0),), MOST)
    center = center.at[:MOST].add(arrived[:MOST])
    center = center.at[own_rows - MOST :].add(arrived[3 * MOST :])
    grad_proj = jnp.concatenate([grad_query, center], axis=1).astype(jnp.bfloat16)
    low_cols = qkv_low.shape[1]
    grad_normed = rows_dot(grad_proj[:, :low_cols], qkv_low) + rows_dot(
        grad_proj[:, low_cols:], qkv_high
    )
    scaled = grad_normed * norm_gain
    grad_unit = (
        scaled
        - jnp.mean(scaled, axis=-1, keepdims=True)
        - unit_rows * jnp.mean(scaled * unit_rows, axis=-1, keepdims=True)
    )
    grad_packed = (grad_rows.astype(jnp.float32) + inv_dev * grad_unit).astype(jnp.bfloat16)
    back_slots = (
        jnp.zeros((groups * slot_count, features), jnp.bfloat16).at[pick_rows].set(grad_packed)
    )
    back_slots = back_slots.reshape(groups, slot_count, features)
    returned = lax.all_to_all(back_slots, DP, split_axis=0, concat_axis=0, tiled=True).reshape(
        groups * slot_count, features
    )
    patch_grad = (
        jnp.zeros((src_count + 1, features), jnp.bfloat16).at[send_flat].add(returned)[:src_count]
    )
    return (layer_out[None], patch_grad[None])


def solution(mesh):
    rows, cols = mesh.devices.shape
    split = Mesh(mesh.devices.reshape(rows // 2, 2, cols), DP + ("tensor",))
    return jax.shard_map(
        local,
        mesh=split,
        in_specs=(
            P(DP, "tensor", None),
            P(DP, "tensor", None, None),
            P(DP, "tensor"),
            P(DP, "tensor"),
            P(),
            P("tensor", None),
            P("tensor", None),
            P(DP, "tensor", None),
        ),
        out_specs=(P(DP, "tensor", None), P(DP, "tensor", None)),
        check_vma=False,
    )
```

```python
import jax
import jax.numpy as jnp
from jax import lax
from jax.sharding import PartitionSpec as P

HD = 112
HEADS = 8
MOST = 96


def extended(block, sides, width):
    for axis, dim in sides:
        count = lax.axis_size(axis)
        forward = [(i, i + 1) for i in range(count - 1)]
        backward = [(target, source) for source, target in forward]
        low = lax.ppermute(
            lax.slice_in_dim(block, block.shape[dim] - width, None, axis=dim), axis, forward
        )
        high = lax.ppermute(lax.slice_in_dim(block, 0, width, axis=dim), axis, backward)
        block = jnp.concatenate([low, block, high], axis=dim)
    return block


def gather_weights(qkv_weight, out_weight):
    qkv_rows, qkv_cols = qkv_weight.shape
    out_rows, out_cols = out_weight.shape
    out_wide = out_weight.reshape(qkv_rows, out_rows * out_cols // qkv_rows)
    both = lax.all_gather(
        jnp.concatenate([qkv_weight, out_wide], axis=1), "tensor", axis=0, tiled=True
    )
    full_qkv = both[:, :qkv_cols]
    out_pairs = both[:, qkv_cols:]
    return full_qkv, out_pairs


def spread(cols, side):
    rows = cols.shape[0]
    none = jnp.zeros_like(cols)
    pair = (cols, none) if side == 0 else (none, cols)
    return jnp.stack(pair, axis=-1).reshape(rows, 2 * cols.shape[1])


def times_out(attended, out_pairs):
    halves = [
        jnp.dot(spread(attended, side), out_pairs, preferred_element_type=jnp.float32)
        for side in range(2)
    ]
    return jnp.concatenate(halves, axis=1)


def times_out_t(grad_rows, out_pairs):
    half = out_pairs.shape[1]
    rows = grad_rows.shape[0]
    parts = [
        lax.dot_general(
            grad_rows[:, side * half : (side + 1) * half],
            out_pairs,
            (((1,), (1,)), ((), ())),
            preferred_element_type=jnp.float32,
        ).reshape(rows, -1, 2)[:, :, side]
        for side in range(2)
    ]
    return parts[0] + parts[1]


def normalize(rows_in, norm_gain):
    values = rows_in.astype(jnp.float32)
    center = values - jnp.mean(values, axis=-1, keepdims=True)
    inv_dev = lax.rsqrt(jnp.mean(center * center, axis=-1, keepdims=True) + 1e-06)
    unit_rows = center * inv_dev
    return (values, unit_rows, inv_dev, (unit_rows * norm_gain).astype(jnp.bfloat16))


def head_blocks(rows_in, count):
    tiled = jnp.tile(rows_in, (HEADS, 1))
    row_head = lax.broadcasted_iota(jnp.int32, tiled.shape, 0) // count
    col_head = lax.broadcasted_iota(jnp.int32, tiled.shape, 1) // HD
    return jnp.where(row_head == col_head, tiled, jnp.zeros_like(tiled))


def own_heads(stacked, count):
    row_head = lax.broadcasted_iota(jnp.int32, stacked.shape, 0) // count
    col_head = lax.broadcasted_iota(jnp.int32, stacked.shape, 1) // HD
    kept = jnp.where(row_head == col_head, stacked, jnp.zeros_like(stacked))
    return kept.reshape(HEADS, count, stacked.shape[1]).sum(axis=0)


def rows_dot(a, b):
    return lax.dot_general(a, b, (((1,), (1,)), ((), ())), preferred_element_type=jnp.float32)


def cols_dot(a, b):
    return lax.dot_general(a, b, (((0,), (0,)), ((), ())), preferred_element_type=jnp.float32)


def attend(queries, keyval, seg_query, seg_key):
    all_heads = HEADS * HD
    score_scale = HD ** (-0.5)
    count = queries.shape[0]
    query_blocks = head_blocks(queries, count)
    scores = rows_dot(query_blocks, keyval[:, :all_heads]) * score_scale
    same_chart = jnp.tile(seg_query[:, None] == seg_key[None, :], (HEADS, 1))
    scores = jnp.where(same_chart, scores, -jnp.inf)
    row_max = jnp.max(scores, axis=1, keepdims=True)
    exp_scores = jnp.exp(scores - row_max)
    row_sum = jnp.sum(exp_scores, axis=1, keepdims=True)
    attn_probs = exp_scores / row_sum
    prob_low = attn_probs.astype(jnp.bfloat16)
    mixed = jnp.dot(prob_low, keyval[:, all_heads:], preferred_element_type=jnp.float32)
    attended = own_heads(mixed, count)
    return (attn_probs, prob_low, attended.astype(jnp.bfloat16), query_blocks)


def local(patch_rows, send_rows, take_rows, segments, norm_gain, qkv_weight, out_weight, grad_out):
    groups = lax.axis_size("dp")
    src_count = patch_rows.shape[1]
    features = patch_rows.shape[2]
    slot_count = send_rows.shape[3]
    own_rows = take_rows.shape[1]
    all_heads = HEADS * HD
    score_scale = HD ** (-0.5)
    patches = patch_rows[0]
    send_flat = send_rows.reshape(groups * slot_count)
    lanes = 128
    outgoing = jnp.take(patches, send_flat, axis=0, mode="fill", fill_value=0).reshape(
        groups, -1, lanes
    )
    incoming = lax.all_to_all(outgoing, "dp", split_axis=0, concat_axis=0, tiled=True).reshape(
        groups * slot_count, features
    )
    pick_rows = take_rows[0]
    slot_total = groups * slot_count
    slot_source = jnp.full((slot_total,), own_rows, jnp.int32).at[pick_rows].set(
        jnp.arange(own_rows, dtype=jnp.int32)
    )
    row_slot = jnp.full((src_count + 1,), slot_total, jnp.int32).at[send_flat].set(
        jnp.arange(slot_total, dtype=jnp.int32)
    )[:src_count]
    packed = jnp.take(incoming, pick_rows, axis=0)
    full_qkv, full_out = gather_weights(qkv_weight, out_weight)
    values, unit_rows, inv_dev, normed = normalize(packed, norm_gain)
    projected = jnp.dot(normed, full_qkv, preferred_element_type=jnp.float32).astype(jnp.bfloat16)
    queries = projected[:, :all_heads]
    keyval = projected[:, all_heads:]
    seg_plus = segments[0] + 1
    wide_kv, wide_seg = (
        extended(keyval, (("tensor", 0),), MOST),
        extended(seg_plus, (("tensor", 0),), MOST),
    )
    attn_probs, prob_low, attended, query_blocks = attend(queries, wide_kv, seg_plus, wide_seg)
    layer_out = (values + times_out(attended, full_out)).astype(jnp.bfloat16)
    grad_rows = grad_out[0]
    grad_att = times_out_t(grad_rows, full_out).astype(jnp.bfloat16)
    grad_blocks = head_blocks(grad_att, own_rows)
    dprobs = rows_dot(grad_blocks, wide_kv[:, all_heads:])
    row_inner = jnp.sum(attn_probs * dprobs, axis=1, keepdims=True)
    dscore = (attn_probs * (dprobs - row_inner) * score_scale).astype(jnp.bfloat16)
    grad_query = own_heads(
        jnp.dot(dscore, wide_kv[:, :all_heads], preferred_element_type=jnp.float32), own_rows
    )
    grad_key = cols_dot(dscore, query_blocks)
    grad_value = cols_dot(prob_low, grad_blocks)
    grad_window = jnp.concatenate([grad_key, grad_value], axis=1)
    center = grad_window[MOST : MOST + own_rows]
    rim_parts = jnp.concatenate([grad_window[:MOST], grad_window[MOST + own_rows :]], axis=0)
    arrived = extended(rim_parts, (("tensor", 0),), MOST)
    center = center.at[:MOST].add(arrived[:MOST])
    center = center.at[own_rows - MOST :].add(arrived[3 * MOST :])
    grad_proj = jnp.concatenate([grad_query, center], axis=1).astype(jnp.bfloat16)
    grad_normed = lax.dot_general(
        grad_proj, full_qkv, (((1,), (1,)), ((), ())), preferred_element_type=jnp.float32
    )
    scaled = grad_normed * norm_gain
    grad_unit = (
        scaled
        - jnp.mean(scaled, axis=-1, keepdims=True)
        - unit_rows * jnp.mean(scaled * unit_rows, axis=-1, keepdims=True)
    )
    grad_packed = (grad_rows.astype(jnp.float32) + inv_dev * grad_unit).astype(jnp.bfloat16)
    back_slots = jnp.take(grad_packed, slot_source, axis=0, mode="fill", fill_value=0)
    back_slots = back_slots.reshape(groups, -1, lanes)
    returned = lax.all_to_all(back_slots, "dp", split_axis=0, concat_axis=0, tiled=True).reshape(
        slot_total, features
    )
    patch_grad = jnp.take(returned, row_slot, axis=0, mode="fill", fill_value=0)
    return (layer_out[None], patch_grad[None])


def solution(mesh):
    return jax.shard_map(
        local,
        mesh=mesh,
        in_specs=(
            P("dp", "tensor", None),
            P("dp", "tensor", None, None),
            P("dp", "tensor"),
            P("dp", "tensor"),
            P(),
            P("tensor", None),
            P("tensor", None),
            P("dp", "tensor", None),
        ),
        out_specs=(P("dp", "tensor", None), P("dp", "tensor", None)),
        check_vma=False,
    )
```

```python
import jax
import jax.numpy as jnp
from jax import lax
from jax.sharding import PartitionSpec as P

HD = 112
HEADS = 8
MOST = 96


def extended(block, sides, width):
    for axis, dim in sides:
        count = lax.axis_size(axis)
        forward = [(i, i + 1) for i in range(count - 1)]
        backward = [(target, source) for source, target in forward]
        low = lax.ppermute(
            lax.slice_in_dim(block, block.shape[dim] - width, None, axis=dim), axis, forward
        )
        high = lax.ppermute(lax.slice_in_dim(block, 0, width, axis=dim), axis, backward)
        block = jnp.concatenate([low, block, high], axis=dim)
    return block


def gather_weights(qkv_weight, out_weight):
    qkv_rows, qkv_cols = qkv_weight.shape
    out_rows, out_cols = out_weight.shape
    out_wide = out_weight.reshape(qkv_rows, out_rows * out_cols // qkv_rows)
    both = lax.all_gather(
        jnp.concatenate([qkv_weight, out_wide], axis=1), "tensor", axis=0, tiled=True
    )
    full_qkv = both[:, :qkv_cols]
    out_pairs = both[:, qkv_cols:]
    return full_qkv, out_pairs


def spread(cols, side):
    rows = cols.shape[0]
    none = jnp.zeros_like(cols)
    pair = (cols, none) if side == 0 else (none, cols)
    return jnp.stack(pair, axis=-1).reshape(rows, 2 * cols.shape[1])


def times_out(attended, out_pairs):
    halves = [
        jnp.dot(spread(attended, side), out_pairs, preferred_element_type=jnp.float32)
        for side in range(2)
    ]
    return jnp.concatenate(halves, axis=1)


def times_out_t(grad_rows, out_pairs):
    half = out_pairs.shape[1]
    rows = grad_rows.shape[0]
    parts = [
        lax.dot_general(
            grad_rows[:, side * half : (side + 1) * half],
            out_pairs,
            (((1,), (1,)), ((), ())),
            preferred_element_type=jnp.float32,
        ).reshape(rows, -1, 2)[:, :, side]
        for side in range(2)
    ]
    return parts[0] + parts[1]


def normalize(rows_in, norm_gain):
    values = rows_in.astype(jnp.float32)
    center = values - jnp.mean(values, axis=-1, keepdims=True)
    inv_dev = lax.rsqrt(jnp.mean(center * center, axis=-1, keepdims=True) + 1e-06)
    unit_rows = center * inv_dev
    return (values, unit_rows, inv_dev, (unit_rows * norm_gain).astype(jnp.bfloat16))


def head_blocks(rows_in, count):
    tiled = jnp.tile(rows_in, (HEADS, 1))
    row_head = lax.broadcasted_iota(jnp.int32, tiled.shape, 0) // count
    col_head = lax.broadcasted_iota(jnp.int32, tiled.shape, 1) // HD
    return jnp.where(row_head == col_head, tiled, jnp.zeros_like(tiled))


def own_heads(stacked, count):
    row_head = lax.broadcasted_iota(jnp.int32, stacked.shape, 0) // count
    col_head = lax.broadcasted_iota(jnp.int32, stacked.shape, 1) // HD
    kept = jnp.where(row_head == col_head, stacked, jnp.zeros_like(stacked))
    return kept.reshape(HEADS, count, stacked.shape[1]).sum(axis=0)


def rows_dot(a, b):
    return lax.dot_general(a, b, (((1,), (1,)), ((), ())), preferred_element_type=jnp.float32)


def cols_dot(a, b):
    return lax.dot_general(a, b, (((0,), (0,)), ((), ())), preferred_element_type=jnp.float32)


def attend(queries, keyval, seg_query, seg_key):
    all_heads = HEADS * HD
    score_scale = HD ** (-0.5)
    count = queries.shape[0]
    query_blocks = head_blocks(queries, count)
    scores = rows_dot(query_blocks, keyval[:, :all_heads]) * score_scale
    same_chart = jnp.tile(seg_query[:, None] == seg_key[None, :], (HEADS, 1))
    scores = jnp.where(same_chart, scores, -jnp.inf)
    row_max = jnp.max(scores, axis=1, keepdims=True)
    exp_scores = jnp.exp(scores - row_max)
    row_sum = jnp.sum(exp_scores, axis=1, keepdims=True)
    attn_probs = exp_scores / row_sum
    prob_low = attn_probs.astype(jnp.bfloat16)
    mixed = jnp.dot(prob_low, keyval[:, all_heads:], preferred_element_type=jnp.float32)
    attended = own_heads(mixed, count)
    return (attn_probs, prob_low, attended.astype(jnp.bfloat16), query_blocks)


def local(patch_rows, send_rows, take_rows, segments, norm_gain, qkv_weight, out_weight, grad_out):
    groups = lax.axis_size("dp")
    src_count = patch_rows.shape[1]
    features = patch_rows.shape[2]
    slot_count = send_rows.shape[3]
    own_rows = take_rows.shape[1]
    all_heads = HEADS * HD
    score_scale = HD ** (-0.5)
    patches = patch_rows[0]
    send_flat = send_rows.reshape(groups * slot_count)
    outgoing = jnp.take(patches, send_flat, axis=0, mode="fill", fill_value=0).reshape(
        groups, slot_count, features
    )
    incoming = lax.all_to_all(outgoing, "dp", split_axis=0, concat_axis=0, tiled=True).reshape(
        groups * slot_count, features
    )
    pick_rows = take_rows[0]
    slot_total = groups * slot_count
    row_slot = jnp.full((src_count + 1,), slot_total, jnp.int32).at[send_flat].set(
        jnp.arange(slot_total, dtype=jnp.int32)
    )[:src_count]
    packed = jnp.take(incoming, pick_rows, axis=0)
    full_qkv, full_out = gather_weights(qkv_weight, out_weight)
    values, unit_rows, inv_dev, normed = normalize(packed, norm_gain)
    projected = jnp.dot(normed, full_qkv, preferred_element_type=jnp.float32).astype(jnp.bfloat16)
    queries = projected[:, :all_heads]
    keyval = projected[:, all_heads:]
    seg_plus = segments[0] + 1
    wide_kv, wide_seg = (
        extended(keyval, (("tensor", 0),), MOST),
        extended(seg_plus, (("tensor", 0),), MOST),
    )
    attn_probs, prob_low, attended, query_blocks = attend(queries, wide_kv, seg_plus, wide_seg)
    layer_out = (values + times_out(attended, full_out)).astype(jnp.bfloat16)
    grad_rows = grad_out[0]
    grad_att = times_out_t(grad_rows, full_out).astype(jnp.bfloat16)
    grad_blocks = head_blocks(grad_att, own_rows)
    dprobs = rows_dot(grad_blocks, wide_kv[:, all_heads:])
    row_inner = jnp.sum(attn_probs * dprobs, axis=1, keepdims=True)
    dscore = (attn_probs * (dprobs - row_inner) * score_scale).astype(jnp.bfloat16)
    grad_query = own_heads(
        jnp.dot(dscore, wide_kv[:, :all_heads], preferred_element_type=jnp.float32), own_rows
    )
    grad_key = cols_dot(dscore, query_blocks)
    grad_value = cols_dot(prob_low, grad_blocks)
    grad_window = jnp.concatenate([grad_key, grad_value], axis=1)
    center = grad_window[MOST : MOST + own_rows]
    rim_parts = jnp.concatenate([grad_window[:MOST], grad_window[MOST + own_rows :]], axis=0)
    arrived = extended(rim_parts, (("tensor", 0),), MOST)
    center = center.at[:MOST].add(arrived[:MOST])
    center = center.at[own_rows - MOST :].add(arrived[3 * MOST :])
    grad_normed = rows_dot(grad_query.astype(jnp.bfloat16), full_qkv[:, :all_heads]) + rows_dot(
        center.astype(jnp.bfloat16), full_qkv[:, all_heads:]
    )
    scaled = grad_normed * norm_gain
    grad_unit = (
        scaled
        - jnp.mean(scaled, axis=-1, keepdims=True)
        - unit_rows * jnp.mean(scaled * unit_rows, axis=-1, keepdims=True)
    )
    grad_packed = (grad_rows.astype(jnp.float32) + inv_dev * grad_unit).astype(jnp.bfloat16)
    back_slots = (
        jnp.zeros((groups, slot_count, features), jnp.bfloat16)
        .at[pick_rows // slot_count, pick_rows % slot_count]
        .set(grad_packed)
    )
    returned = lax.all_to_all(back_slots, "dp", split_axis=0, concat_axis=0, tiled=True)
    patch_grad = returned.at[row_slot // slot_count, row_slot % slot_count].get(
        mode="fill", fill_value=0
    )
    return (layer_out[None], patch_grad[None])


def solution(mesh):
    return jax.shard_map(
        local,
        mesh=mesh,
        in_specs=(
            P("dp", "tensor", None),
            P("dp", "tensor", None, None),
            P("dp", "tensor"),
            P("dp", "tensor"),
            P(),
            P("tensor", None),
            P("tensor", None),
            P("dp", "tensor", None),
        ),
        out_specs=(P("dp", "tensor", None), P("dp", "tensor", None)),
        check_vma=False,
    )
```

```python
import jax
import jax.numpy as jnp
from jax import lax
from jax.sharding import PartitionSpec as P

HD = 112
HEADS = 8
MOST = 96


def extended(block, sides, width):
    for axis, dim in sides:
        count = lax.axis_size(axis)
        forward = [(i, i + 1) for i in range(count - 1)]
        backward = [(target, source) for source, target in forward]
        low = lax.ppermute(
            lax.slice_in_dim(block, block.shape[dim] - width, None, axis=dim), axis, forward
        )
        high = lax.ppermute(lax.slice_in_dim(block, 0, width, axis=dim), axis, backward)
        block = jnp.concatenate([low, block, high], axis=dim)
    return block


def gather_weights(qkv_weight, out_weight):
    qkv_rows, qkv_cols = qkv_weight.shape
    out_rows, out_cols = out_weight.shape
    out_wide = out_weight.reshape(qkv_rows, out_rows * out_cols // qkv_rows)
    both = lax.all_gather(
        jnp.concatenate([qkv_weight, out_wide], axis=1), "tensor", axis=0, tiled=True
    )
    full_qkv = both[:, :qkv_cols]
    out_pairs = both[:, qkv_cols:]
    return full_qkv, out_pairs


def spread(cols, side):
    rows = cols.shape[0]
    none = jnp.zeros_like(cols)
    pair = (cols, none) if side == 0 else (none, cols)
    return jnp.stack(pair, axis=-1).reshape(rows, 2 * cols.shape[1])


def times_out(attended, out_pairs):
    halves = [
        jnp.dot(spread(attended, side), out_pairs, preferred_element_type=jnp.float32)
        for side in range(2)
    ]
    return jnp.concatenate(halves, axis=1)


def times_out_t(grad_rows, out_pairs):
    half = out_pairs.shape[1]
    rows = grad_rows.shape[0]
    parts = [
        lax.dot_general(
            grad_rows[:, side * half : (side + 1) * half],
            out_pairs,
            (((1,), (1,)), ((), ())),
            preferred_element_type=jnp.float32,
        ).reshape(rows, -1, 2)[:, :, side]
        for side in range(2)
    ]
    return parts[0] + parts[1]


def normalize(rows_in, norm_gain):
    values = rows_in.astype(jnp.float32)
    center = values - jnp.mean(values, axis=-1, keepdims=True)
    inv_dev = lax.rsqrt(jnp.mean(center * center, axis=-1, keepdims=True) + 1e-06)
    unit_rows = center * inv_dev
    return (values, unit_rows, inv_dev, (unit_rows * norm_gain).astype(jnp.bfloat16))


def head_blocks(rows_in, count):
    tiled = jnp.tile(rows_in, (HEADS, 1))
    row_head = lax.broadcasted_iota(jnp.int32, tiled.shape, 0) // count
    col_head = lax.broadcasted_iota(jnp.int32, tiled.shape, 1) // HD
    return jnp.where(row_head == col_head, tiled, jnp.zeros_like(tiled))


def own_heads(stacked, count):
    row_head = lax.broadcasted_iota(jnp.int32, stacked.shape, 0) // count
    col_head = lax.broadcasted_iota(jnp.int32, stacked.shape, 1) // HD
    kept = jnp.where(row_head == col_head, stacked, jnp.zeros_like(stacked))
    return kept.reshape(HEADS, count, stacked.shape[1]).sum(axis=0)


def rows_dot(a, b):
    return lax.dot_general(a, b, (((1,), (1,)), ((), ())), preferred_element_type=jnp.float32)


def cols_dot(a, b):
    return lax.dot_general(a, b, (((0,), (0,)), ((), ())), preferred_element_type=jnp.float32)


def attend(queries, keyval, seg_query, seg_key):
    all_heads = HEADS * HD
    score_scale = HD ** (-0.5)
    count = queries.shape[0]
    query_blocks = head_blocks(queries, count)
    scores = rows_dot(query_blocks, keyval[:, :all_heads]) * score_scale
    same_chart = jnp.tile(seg_query[:, None] == seg_key[None, :], (HEADS, 1))
    scores = jnp.where(same_chart, scores, -jnp.inf)
    row_max = jnp.max(scores, axis=1, keepdims=True)
    exp_scores = jnp.exp(scores - row_max)
    row_sum = jnp.sum(exp_scores, axis=1, keepdims=True)
    attn_probs = exp_scores / row_sum
    prob_low = attn_probs.astype(jnp.bfloat16)
    mixed = jnp.dot(prob_low, keyval[:, all_heads:], preferred_element_type=jnp.float32)
    attended = own_heads(mixed, count)
    return (attn_probs, prob_low, attended.astype(jnp.bfloat16), query_blocks)


def local(patch_rows, send_rows, take_rows, segments, norm_gain, qkv_weight, out_weight, grad_out):
    groups = lax.axis_size("dp")
    src_count = patch_rows.shape[1]
    features = patch_rows.shape[2]
    slot_count = send_rows.shape[3]
    own_rows = take_rows.shape[1]
    all_heads = HEADS * HD
    score_scale = HD ** (-0.5)
    patches = patch_rows[0]
    send_flat = send_rows.reshape(groups * slot_count)
    outgoing = jnp.take(patches, send_flat, axis=0, mode="fill", fill_value=0).reshape(
        groups, slot_count, features
    )
    incoming = lax.all_to_all(outgoing, "dp", split_axis=0, concat_axis=0, tiled=True).reshape(
        groups * slot_count, features
    )
    pick_rows = take_rows[0]
    slot_total = groups * slot_count
    row_slot = jnp.full((src_count + 1,), slot_total, jnp.int32).at[send_flat].set(
        jnp.arange(slot_total, dtype=jnp.int32)
    )[:src_count]
    packed = jnp.take(incoming, pick_rows, axis=0)
    full_qkv, full_out = gather_weights(qkv_weight, out_weight)
    values, unit_rows, inv_dev, normed = normalize(packed, norm_gain)
    projected = jnp.dot(normed, full_qkv, preferred_element_type=jnp.float32).astype(jnp.bfloat16)
    queries = projected[:, :all_heads]
    keyval = projected[:, all_heads:]
    seg_plus = segments[0] + 1
    wide_kv, wide_seg = (
        extended(keyval, (("tensor", 0),), MOST),
        extended(seg_plus, (("tensor", 0),), MOST),
    )
    attn_probs, prob_low, attended, query_blocks = attend(queries, wide_kv, seg_plus, wide_seg)
    layer_out = (values + times_out(attended, full_out)).astype(jnp.bfloat16)
    grad_rows = grad_out[0]
    grad_att = times_out_t(grad_rows, full_out).astype(jnp.bfloat16)
    grad_blocks = head_blocks(grad_att, own_rows)
    dprobs = rows_dot(grad_blocks, wide_kv[:, all_heads:])
    row_inner = jnp.sum(attn_probs * dprobs, axis=1, keepdims=True)
    dscore = (attn_probs * (dprobs - row_inner) * score_scale).astype(jnp.bfloat16)
    grad_query = own_heads(
        jnp.dot(dscore, wide_kv[:, :all_heads], preferred_element_type=jnp.float32), own_rows
    )
    grad_key = cols_dot(dscore, query_blocks)
    grad_value = cols_dot(prob_low, grad_blocks)
    grad_window = jnp.concatenate([grad_key, grad_value], axis=1)
    center = grad_window[MOST : MOST + own_rows]
    rim_parts = jnp.concatenate([grad_window[:MOST], grad_window[MOST + own_rows :]], axis=0)
    arrived = extended(rim_parts, (("tensor", 0),), MOST)
    center = center.at[:MOST].add(arrived[:MOST])
    center = center.at[own_rows - MOST :].add(arrived[3 * MOST :])
    grad_normed = rows_dot(grad_query.astype(jnp.bfloat16), full_qkv[:, :all_heads]) + rows_dot(
        center.astype(jnp.bfloat16), full_qkv[:, all_heads:]
    )
    scaled = grad_normed * norm_gain
    grad_unit = (
        scaled
        - jnp.mean(scaled, axis=-1, keepdims=True)
        - unit_rows * jnp.mean(scaled * unit_rows, axis=-1, keepdims=True)
    )
    grad_packed = (grad_rows.astype(jnp.float32) + inv_dev * grad_unit).astype(jnp.bfloat16)
    back_slots = (
        jnp.zeros((groups * slot_count, features), jnp.bfloat16).at[pick_rows].set(grad_packed)
    )
    back_slots = back_slots.reshape(groups, slot_count, features)
    returned = lax.all_to_all(back_slots, "dp", split_axis=0, concat_axis=0, tiled=True).reshape(
        groups * slot_count, features
    )
    patch_grad = jnp.take(returned, row_slot, axis=0, mode="fill", fill_value=0)
    return (layer_out[None], patch_grad[None])


def solution(mesh):
    return jax.shard_map(
        local,
        mesh=mesh,
        in_specs=(
            P("dp", "tensor", None),
            P("dp", "tensor", None, None),
            P("dp", "tensor"),
            P("dp", "tensor"),
            P(),
            P("tensor", None),
            P("tensor", None),
            P("dp", "tensor", None),
        ),
        out_specs=(P("dp", "tensor", None), P("dp", "tensor", None)),
        check_vma=False,
    )
```

```python
import jax
import jax.numpy as jnp
from jax import lax
from jax.sharding import PartitionSpec as P

HD = 112
HEADS = 8
MOST = 96


def extended(block, sides, width):
    for axis, dim in sides:
        count = lax.axis_size(axis)
        forward = [(i, i + 1) for i in range(count - 1)]
        backward = [(target, source) for source, target in forward]
        low = lax.ppermute(
            lax.slice_in_dim(block, block.shape[dim] - width, None, axis=dim), axis, forward
        )
        high = lax.ppermute(lax.slice_in_dim(block, 0, width, axis=dim), axis, backward)
        block = jnp.concatenate([low, block, high], axis=dim)
    return block


def gather_weights(qkv_weight, out_weight):
    qkv_rows, qkv_cols = qkv_weight.shape
    out_rows, out_cols = out_weight.shape
    out_wide = out_weight.reshape(qkv_rows, out_rows * out_cols // qkv_rows)
    both = lax.all_gather(
        jnp.concatenate([qkv_weight, out_wide], axis=1), "tensor", axis=0, tiled=True
    )
    full_qkv = both[:, :qkv_cols]
    out_pairs = both[:, qkv_cols:]
    return full_qkv, out_pairs


def spread(cols, side):
    rows = cols.shape[0]
    none = jnp.zeros_like(cols)
    pair = (cols, none) if side == 0 else (none, cols)
    return jnp.stack(pair, axis=-1).reshape(rows, 2 * cols.shape[1])


def times_out(attended, out_pairs):
    halves = [
        jnp.dot(spread(attended, side), out_pairs, preferred_element_type=jnp.float32)
        for side in range(2)
    ]
    return jnp.concatenate(halves, axis=1)


def times_out_t(grad_rows, out_pairs):
    half = out_pairs.shape[1]
    rows = grad_rows.shape[0]
    parts = [
        lax.dot_general(
            grad_rows[:, side * half : (side + 1) * half],
            out_pairs,
            (((1,), (1,)), ((), ())),
            preferred_element_type=jnp.float32,
        ).reshape(rows, -1, 2)[:, :, side]
        for side in range(2)
    ]
    return parts[0] + parts[1]


def normalize(rows_in, norm_gain):
    values = rows_in.astype(jnp.float32)
    center = values - jnp.mean(values, axis=-1, keepdims=True)
    inv_dev = lax.rsqrt(jnp.mean(center * center, axis=-1, keepdims=True) + 1e-06)
    unit_rows = center * inv_dev
    return (values, unit_rows, inv_dev, (unit_rows * norm_gain).astype(jnp.bfloat16))


def head_blocks(rows_in, count):
    tiled = jnp.tile(rows_in, (HEADS, 1))
    row_head = lax.broadcasted_iota(jnp.int32, tiled.shape, 0) // count
    col_head = lax.broadcasted_iota(jnp.int32, tiled.shape, 1) // HD
    return jnp.where(row_head == col_head, tiled, jnp.zeros_like(tiled))


def own_heads(stacked, count):
    row_head = lax.broadcasted_iota(jnp.int32, stacked.shape, 0) // count
    col_head = lax.broadcasted_iota(jnp.int32, stacked.shape, 1) // HD
    kept = jnp.where(row_head == col_head, stacked, jnp.zeros_like(stacked))
    return kept.reshape(HEADS, count, stacked.shape[1]).sum(axis=0)


def rows_dot(a, b):
    return lax.dot_general(a, b, (((1,), (1,)), ((), ())), preferred_element_type=jnp.float32)


def cols_dot(a, b):
    return lax.dot_general(a, b, (((0,), (0,)), ((), ())), preferred_element_type=jnp.float32)


def attend(queries, keyval, seg_query, seg_key):
    all_heads = HEADS * HD
    score_scale = HD ** (-0.5)
    count = queries.shape[0]
    query_blocks = head_blocks(queries, count)
    scores = rows_dot(query_blocks, keyval[:, :all_heads]) * score_scale
    same_chart = jnp.tile(seg_query[:, None] == seg_key[None, :], (HEADS, 1))
    scores = jnp.where(same_chart, scores, -jnp.inf)
    row_max = jnp.max(scores, axis=1, keepdims=True)
    exp_scores = jnp.exp(scores - row_max)
    row_sum = jnp.sum(exp_scores, axis=1, keepdims=True)
    attn_probs = exp_scores / row_sum
    prob_low = attn_probs.astype(jnp.bfloat16)
    mixed = jnp.dot(prob_low, keyval[:, all_heads:], preferred_element_type=jnp.float32)
    attended = own_heads(mixed, count)
    return (attn_probs, prob_low, attended.astype(jnp.bfloat16), query_blocks)


def local(patch_rows, send_rows, take_rows, segments, norm_gain, qkv_weight, out_weight, grad_out):
    groups = lax.axis_size("dp")
    src_count = patch_rows.shape[1]
    features = patch_rows.shape[2]
    slot_count = send_rows.shape[3]
    own_rows = take_rows.shape[1]
    all_heads = HEADS * HD
    score_scale = HD ** (-0.5)
    patches = patch_rows[0]
    send_flat = send_rows.reshape(groups * slot_count)
    outgoing = jnp.take(patches, send_flat, axis=0, mode="fill", fill_value=0).reshape(
        groups, slot_count, features
    )
    incoming = lax.all_to_all(outgoing, "dp", split_axis=0, concat_axis=0, tiled=True).reshape(
        groups * slot_count, features
    )
    pick_rows = take_rows[0]
    packed = jnp.take(incoming, pick_rows, axis=0)
    full_qkv, full_out = gather_weights(qkv_weight, out_weight)
    values, unit_rows, inv_dev, normed = normalize(packed, norm_gain)
    projected = jnp.dot(normed, full_qkv, preferred_element_type=jnp.float32).astype(jnp.bfloat16)
    queries = projected[:, :all_heads]
    keyval = projected[:, all_heads:]
    seg_plus = segments[0] + 1
    wide_kv, wide_seg = (
        extended(keyval, (("tensor", 0),), MOST),
        extended(seg_plus, (("tensor", 0),), MOST),
    )
    attn_probs, prob_low, attended, query_blocks = attend(queries, wide_kv, seg_plus, wide_seg)
    layer_out = (values + times_out(attended, full_out)).astype(jnp.bfloat16)
    grad_rows = grad_out[0]
    grad_att = times_out_t(grad_rows, full_out).astype(jnp.bfloat16)
    grad_blocks = head_blocks(grad_att, own_rows)
    dprobs = rows_dot(grad_blocks, wide_kv[:, all_heads:])
    row_inner = jnp.sum(attn_probs * dprobs, axis=1, keepdims=True)
    dscore = (attn_probs * (dprobs - row_inner) * score_scale).astype(jnp.bfloat16)
    window_rows = wide_kv.shape[0]
    score_rows = dscore.reshape(HEADS, own_rows, window_rows).transpose(1, 0, 2)
    grad_query = jnp.dot(
        score_rows.reshape(own_rows, HEADS * window_rows),
        head_blocks(wide_kv[:, :all_heads], window_rows),
        preferred_element_type=jnp.float32,
    )
    grad_key = cols_dot(dscore, query_blocks)
    grad_value = cols_dot(prob_low, grad_blocks)
    grad_window = jnp.concatenate([grad_key, grad_value], axis=1)
    center = grad_window[MOST : MOST + own_rows]
    rim_parts = jnp.concatenate([grad_window[:MOST], grad_window[MOST + own_rows :]], axis=0)
    arrived = extended(rim_parts, (("tensor", 0),), MOST)
    center = center.at[:MOST].add(arrived[:MOST])
    center = center.at[own_rows - MOST :].add(arrived[3 * MOST :])
    grad_proj = jnp.concatenate([grad_query, center], axis=1).astype(jnp.bfloat16)
    grad_normed = lax.dot_general(
        grad_proj, full_qkv, (((1,), (1,)), ((), ())), preferred_element_type=jnp.float32
    )
    scaled = grad_normed * norm_gain
    grad_unit = (
        scaled
        - jnp.mean(scaled, axis=-1, keepdims=True)
        - unit_rows * jnp.mean(scaled * unit_rows, axis=-1, keepdims=True)
    )
    grad_packed = (grad_rows.astype(jnp.float32) + inv_dev * grad_unit).astype(jnp.bfloat16)
    back_slots = (
        jnp.zeros((groups * slot_count, features), jnp.bfloat16).at[pick_rows].set(grad_packed)
    )
    back_slots = back_slots.reshape(groups, slot_count, features)
    returned = lax.all_to_all(back_slots, "dp", split_axis=0, concat_axis=0, tiled=True).reshape(
        groups * slot_count, features
    )
    patch_grad = (
        jnp.zeros((src_count + 1, features), jnp.bfloat16).at[send_flat].add(returned)[:src_count]
    )
    return (layer_out[None], patch_grad[None])


def solution(mesh):
    return jax.shard_map(
        local,
        mesh=mesh,
        in_specs=(
            P("dp", "tensor", None),
            P("dp", "tensor", None, None),
            P("dp", "tensor"),
            P("dp", "tensor"),
            P(),
            P("tensor", None),
            P("tensor", None),
            P("dp", "tensor", None),
        ),
        out_specs=(P("dp", "tensor", None), P("dp", "tensor", None)),
        check_vma=False,
    )
```

```python
import jax
import jax.numpy as jnp
from jax import lax
from jax.sharding import PartitionSpec as P

HD = 112
HEADS = 8
MOST = 96


def extended(block, sides, width):
    for axis, dim in sides:
        count = lax.axis_size(axis)
        forward = [(i, i + 1) for i in range(count - 1)]
        backward = [(target, source) for source, target in forward]
        low = lax.ppermute(
            lax.slice_in_dim(block, block.shape[dim] - width, None, axis=dim), axis, forward
        )
        high = lax.ppermute(lax.slice_in_dim(block, 0, width, axis=dim), axis, backward)
        block = jnp.concatenate([low, block, high], axis=dim)
    return block


def gather_weights(qkv_weight, out_weight):
    qkv_rows, qkv_cols = qkv_weight.shape
    out_rows, out_cols = out_weight.shape
    out_wide = out_weight.reshape(qkv_rows, out_rows * out_cols // qkv_rows)
    both = lax.all_gather(
        jnp.concatenate([qkv_weight, out_wide], axis=1), "tensor", axis=0, tiled=True
    )
    full_qkv = both[:, :qkv_cols]
    out_pairs = both[:, qkv_cols:]
    return full_qkv, out_pairs


def spread(cols, side):
    rows = cols.shape[0]
    none = jnp.zeros_like(cols)
    pair = (cols, none) if side == 0 else (none, cols)
    return jnp.stack(pair, axis=-1).reshape(rows, 2 * cols.shape[1])


def times_out(attended, out_pairs):
    halves = [
        jnp.dot(spread(attended, side), out_pairs, preferred_element_type=jnp.float32)
        for side in range(2)
    ]
    return jnp.concatenate(halves, axis=1)


def times_out_t(grad_rows, out_pairs):
    half = out_pairs.shape[1]
    rows = grad_rows.shape[0]
    parts = [
        lax.dot_general(
            grad_rows[:, side * half : (side + 1) * half],
            out_pairs,
            (((1,), (1,)), ((), ())),
            preferred_element_type=jnp.float32,
        ).reshape(rows, -1, 2)[:, :, side]
        for side in range(2)
    ]
    return parts[0] + parts[1]


def normalize(rows_in, norm_gain):
    values = rows_in.astype(jnp.float32)
    center = values - jnp.mean(values, axis=-1, keepdims=True)
    inv_dev = lax.rsqrt(jnp.mean(center * center, axis=-1, keepdims=True) + 1e-06)
    unit_rows = center * inv_dev
    return (values, unit_rows, inv_dev, (unit_rows * norm_gain).astype(jnp.bfloat16))


def head_blocks(rows_in, count):
    tiled = jnp.tile(rows_in, (HEADS, 1))
    row_head = lax.broadcasted_iota(jnp.int32, tiled.shape, 0) // count
    col_head = lax.broadcasted_iota(jnp.int32, tiled.shape, 1) // HD
    return jnp.where(row_head == col_head, tiled, jnp.zeros_like(tiled))


def own_heads(stacked, count):
    row_head = lax.broadcasted_iota(jnp.int32, stacked.shape, 0) // count
    col_head = lax.broadcasted_iota(jnp.int32, stacked.shape, 1) // HD
    kept = jnp.where(row_head == col_head, stacked, jnp.zeros_like(stacked))
    return kept.reshape(HEADS, count, stacked.shape[1]).sum(axis=0)


def rows_dot(a, b):
    return lax.dot_general(a, b, (((1,), (1,)), ((), ())), preferred_element_type=jnp.float32)


def cols_dot(a, b):
    return lax.dot_general(a, b, (((0,), (0,)), ((), ())), preferred_element_type=jnp.float32)


def attend(queries, keyval, seg_query, seg_key):
    all_heads = HEADS * HD
    score_scale = HD ** (-0.5)
    count = queries.shape[0]
    query_blocks = head_blocks(queries, count)
    scores = rows_dot(query_blocks, keyval[:, :all_heads]) * score_scale
    same_chart = jnp.tile(seg_query[:, None] == seg_key[None, :], (HEADS, 1))
    scores = jnp.where(same_chart, scores, -jnp.inf)
    row_max = jnp.max(scores, axis=1, keepdims=True)
    exp_scores = jnp.exp(scores - row_max)
    row_sum = jnp.sum(exp_scores, axis=1, keepdims=True)
    attn_probs = exp_scores / row_sum
    prob_low = attn_probs.astype(jnp.bfloat16)
    mixed = jnp.dot(prob_low, keyval[:, all_heads:], preferred_element_type=jnp.float32)
    attended = own_heads(mixed, count)
    return (attn_probs, prob_low, attended.astype(jnp.bfloat16), query_blocks)


def local(patch_rows, send_rows, take_rows, segments, norm_gain, qkv_weight, out_weight, grad_out):
    groups = lax.axis_size("dp")
    src_count = patch_rows.shape[1]
    features = patch_rows.shape[2]
    slot_count = send_rows.shape[3]
    own_rows = take_rows.shape[1]
    all_heads = HEADS * HD
    score_scale = HD ** (-0.5)
    patches = patch_rows[0]
    send_flat = send_rows.reshape(groups * slot_count)
    outgoing = jnp.take(patches, send_flat, axis=0, mode="fill", fill_value=0).reshape(
        groups, slot_count, features
    )
    incoming = lax.all_to_all(outgoing, "dp", split_axis=0, concat_axis=0, tiled=True).reshape(
        groups * slot_count, features
    )
    pick_rows = take_rows[0]
    slot_total = groups * slot_count
    row_slot = jnp.full((src_count + 1,), slot_total, jnp.int32).at[send_flat].set(
        jnp.arange(slot_total, dtype=jnp.int32)
    )[:src_count]
    packed = jnp.take(incoming, pick_rows, axis=0)
    full_qkv, full_out = gather_weights(qkv_weight, out_weight)
    values, unit_rows, inv_dev, normed = normalize(packed, norm_gain)
    projected = jnp.dot(normed, full_qkv, preferred_element_type=jnp.float32).astype(jnp.bfloat16)
    queries = projected[:, :all_heads]
    keyval = projected[:, all_heads:]
    seg_plus = segments[0] + 1
    wide_kv, wide_seg = (
        extended(keyval, (("tensor", 0),), MOST),
        extended(seg_plus, (("tensor", 0),), MOST),
    )
    attn_probs, prob_low, attended, query_blocks = attend(queries, wide_kv, seg_plus, wide_seg)
    layer_out = (values + times_out(attended, full_out)).astype(jnp.bfloat16)
    grad_rows = grad_out[0]
    grad_att = times_out_t(grad_rows, full_out).astype(jnp.bfloat16)
    grad_blocks = head_blocks(grad_att, own_rows)
    dprobs = rows_dot(grad_blocks, wide_kv[:, all_heads:])
    row_inner = jnp.sum(attn_probs * dprobs, axis=1, keepdims=True)
    dscore = (attn_probs * (dprobs - row_inner) * score_scale).astype(jnp.bfloat16)
    window_rows = wide_kv.shape[0]
    score_rows = dscore.reshape(HEADS, own_rows, window_rows).transpose(1, 0, 2)
    grad_query = jnp.dot(
        score_rows.reshape(own_rows, HEADS * window_rows),
        head_blocks(wide_kv[:, :all_heads], window_rows),
        preferred_element_type=jnp.float32,
    )
    grad_key = cols_dot(dscore, query_blocks)
    grad_value = cols_dot(prob_low, grad_blocks)
    grad_window = jnp.concatenate([grad_key, grad_value], axis=1)
    center = grad_window[MOST : MOST + own_rows]
    rim_parts = jnp.concatenate([grad_window[:MOST], grad_window[MOST + own_rows :]], axis=0)
    arrived = extended(rim_parts, (("tensor", 0),), MOST)
    center = center.at[:MOST].add(arrived[:MOST])
    center = center.at[own_rows - MOST :].add(arrived[3 * MOST :])
    grad_proj = jnp.concatenate([grad_query, center], axis=1).astype(jnp.bfloat16)
    grad_normed = lax.dot_general(
        grad_proj, full_qkv, (((1,), (1,)), ((), ())), preferred_element_type=jnp.float32
    )
    scaled = grad_normed * norm_gain
    grad_unit = (
        scaled
        - jnp.mean(scaled, axis=-1, keepdims=True)
        - unit_rows * jnp.mean(scaled * unit_rows, axis=-1, keepdims=True)
    )
    grad_packed = (grad_rows.astype(jnp.float32) + inv_dev * grad_unit).astype(jnp.bfloat16)
    back_slots = (
        jnp.zeros((groups * slot_count, features), jnp.bfloat16).at[pick_rows].set(grad_packed)
    )
    back_slots = back_slots.reshape(groups, slot_count, features)
    returned = lax.all_to_all(back_slots, "dp", split_axis=0, concat_axis=0, tiled=True).reshape(
        groups * slot_count, features
    )
    patch_grad = jnp.take(returned, row_slot, axis=0, mode="fill", fill_value=0)
    return (layer_out[None], patch_grad[None])


def solution(mesh):
    return jax.shard_map(
        local,
        mesh=mesh,
        in_specs=(
            P("dp", "tensor", None),
            P("dp", "tensor", None, None),
            P("dp", "tensor"),
            P("dp", "tensor"),
            P(),
            P("tensor", None),
            P("tensor", None),
            P("dp", "tensor", None),
        ),
        out_specs=(P("dp", "tensor", None), P("dp", "tensor", None)),
        check_vma=False,
    )
```

```python
import jax
import jax.numpy as jnp
from jax import lax
from jax.sharding import PartitionSpec as P

HD = 112
HEADS = 8
MOST = 96


def extended(block, sides, width):
    for axis, dim in sides:
        count = lax.axis_size(axis)
        forward = [(i, i + 1) for i in range(count - 1)]
        backward = [(target, source) for source, target in forward]
        low = lax.ppermute(
            lax.slice_in_dim(block, block.shape[dim] - width, None, axis=dim), axis, forward
        )
        high = lax.ppermute(lax.slice_in_dim(block, 0, width, axis=dim), axis, backward)
        block = jnp.concatenate([low, block, high], axis=dim)
    return block


def gather_weights(qkv_weight, out_weight):
    qkv_rows, qkv_cols = qkv_weight.shape
    out_rows, out_cols = out_weight.shape
    out_wide = out_weight.reshape(qkv_rows, out_rows * out_cols // qkv_rows)
    both = lax.all_gather(
        jnp.concatenate([qkv_weight, out_wide], axis=1), "tensor", axis=0, tiled=True
    )
    full_qkv = both[:, :qkv_cols]
    out_pairs = both[:, qkv_cols:]
    return full_qkv, out_pairs


def spread(cols, side):
    rows = cols.shape[0]
    none = jnp.zeros_like(cols)
    pair = (cols, none) if side == 0 else (none, cols)
    return jnp.stack(pair, axis=-1).reshape(rows, 2 * cols.shape[1])


def times_out(attended, out_pairs):
    halves = [
        jnp.dot(spread(attended, side), out_pairs, preferred_element_type=jnp.float32)
        for side in range(2)
    ]
    return jnp.concatenate(halves, axis=1)


def times_out_t(grad_rows, out_pairs):
    half = out_pairs.shape[1]
    rows = grad_rows.shape[0]
    parts = [
        lax.dot_general(
            grad_rows[:, side * half : (side + 1) * half],
            out_pairs,
            (((1,), (1,)), ((), ())),
            preferred_element_type=jnp.float32,
        ).reshape(rows, -1, 2)[:, :, side]
        for side in range(2)
    ]
    return parts[0] + parts[1]


def normalize(rows_in, norm_gain):
    values = rows_in.astype(jnp.float32)
    center = values - jnp.mean(values, axis=-1, keepdims=True)
    inv_dev = lax.rsqrt(jnp.mean(center * center, axis=-1, keepdims=True) + 1e-06)
    unit_rows = center * inv_dev
    return (values, unit_rows, inv_dev, (unit_rows * norm_gain).astype(jnp.bfloat16))


def head_blocks(rows_in, count):
    tiled = jnp.tile(rows_in, (HEADS, 1))
    row_head = lax.broadcasted_iota(jnp.int32, tiled.shape, 0) // count
    col_head = lax.broadcasted_iota(jnp.int32, tiled.shape, 1) // HD
    return jnp.where(row_head == col_head, tiled, jnp.zeros_like(tiled))


def own_heads(stacked, count):
    row_head = lax.broadcasted_iota(jnp.int32, stacked.shape, 0) // count
    col_head = lax.broadcasted_iota(jnp.int32, stacked.shape, 1) // HD
    kept = jnp.where(row_head == col_head, stacked, jnp.zeros_like(stacked))
    return kept.reshape(HEADS, count, stacked.shape[1]).sum(axis=0)


def rows_dot(a, b):
    return lax.dot_general(a, b, (((1,), (1,)), ((), ())), preferred_element_type=jnp.float32)


def cols_dot(a, b):
    return lax.dot_general(a, b, (((0,), (0,)), ((), ())), preferred_element_type=jnp.float32)


def attend(queries, keyval, seg_query, seg_key):
    all_heads = HEADS * HD
    score_scale = HD ** (-0.5)
    count = queries.shape[0]
    query_blocks = head_blocks(queries, count)
    scores = rows_dot(query_blocks, keyval[:, :all_heads]) * score_scale
    same_chart = jnp.tile(seg_query[:, None] == seg_key[None, :], (HEADS, 1))
    scores = jnp.where(same_chart, scores, -jnp.inf)
    row_max = jnp.max(scores, axis=1, keepdims=True)
    exp_scores = jnp.exp(scores - row_max)
    row_sum = jnp.sum(exp_scores, axis=1, keepdims=True)
    attn_probs = exp_scores / row_sum
    prob_low = attn_probs.astype(jnp.bfloat16)
    mixed = jnp.dot(prob_low, keyval[:, all_heads:], preferred_element_type=jnp.float32)
    attended = own_heads(mixed, count)
    return (attn_probs, prob_low, attended.astype(jnp.bfloat16), query_blocks)


def local(patch_rows, send_rows, take_rows, segments, norm_gain, qkv_weight, out_weight, grad_out):
    groups = lax.axis_size("dp")
    src_count = patch_rows.shape[1]
    features = patch_rows.shape[2]
    slot_count = send_rows.shape[3]
    own_rows = take_rows.shape[1]
    all_heads = HEADS * HD
    score_scale = HD ** (-0.5)
    patches = patch_rows[0]
    send_flat = send_rows.reshape(groups * slot_count)
    outgoing = jnp.take(patches, send_flat, axis=0, mode="fill", fill_value=0).reshape(
        groups, slot_count, features
    )
    incoming = lax.all_to_all(outgoing, "dp", split_axis=0, concat_axis=0, tiled=True).reshape(
        groups * slot_count, features
    )
    pick_rows = take_rows[0]
    slot_total = groups * slot_count
    row_slot = jnp.full((src_count + 1,), slot_total, jnp.int32).at[send_flat].set(
        jnp.arange(slot_total, dtype=jnp.int32)
    )[:src_count]
    packed = jnp.take(incoming, pick_rows, axis=0)
    full_qkv, full_out = gather_weights(qkv_weight, out_weight)
    values, unit_rows, inv_dev, normed = normalize(packed, norm_gain)
    projected = jnp.dot(normed, full_qkv, preferred_element_type=jnp.float32).astype(jnp.bfloat16)
    queries = projected[:, :all_heads]
    keyval = projected[:, all_heads:]
    seg_plus = segments[0] + 1
    wide_kv, wide_seg = (
        extended(keyval, (("tensor", 0),), MOST),
        extended(seg_plus, (("tensor", 0),), MOST),
    )
    attn_probs, prob_low, attended, query_blocks = attend(queries, wide_kv, seg_plus, wide_seg)
    layer_out = (values + times_out(attended, full_out)).astype(jnp.bfloat16)
    grad_rows = grad_out[0]
    grad_att = times_out_t(grad_rows, full_out).astype(jnp.bfloat16)
    grad_blocks = head_blocks(grad_att, own_rows)
    dprobs = rows_dot(grad_blocks, wide_kv[:, all_heads:])
    row_inner = jnp.sum(attn_probs * dprobs, axis=1, keepdims=True)
    dscore = (attn_probs * (dprobs - row_inner) * score_scale).astype(jnp.bfloat16)
    window_rows = wide_kv.shape[0]
    score_rows = dscore.reshape(HEADS, own_rows, window_rows).transpose(1, 0, 2)
    grad_query = jnp.dot(
        score_rows.reshape(own_rows, HEADS * window_rows),
        head_blocks(wide_kv[:, :all_heads], window_rows),
        preferred_element_type=jnp.float32,
    )
    grad_key = cols_dot(dscore, query_blocks)
    grad_value = cols_dot(prob_low, grad_blocks)
    grad_window = jnp.concatenate([grad_key, grad_value], axis=1)
    center = grad_window[MOST : MOST + own_rows]
    blocks = lax.axis_size("tensor")
    ahead = [(i, i + 1) for i in range(blocks - 1)]
    behind = [(target, source) for source, target in ahead]
    high_rim, low_rim = lax.optimization_barrier((grad_window[MOST + own_rows :], grad_window[:MOST]))
    from_prev = lax.ppermute(high_rim, "tensor", ahead)
    from_next = lax.ppermute(low_rim, "tensor", behind)
    center = center.at[:MOST].add(from_prev)
    center = center.at[own_rows - MOST :].add(from_next)
    grad_proj = jnp.concatenate([grad_query, center], axis=1).astype(jnp.bfloat16)
    grad_normed = lax.dot_general(
        grad_proj, full_qkv, (((1,), (1,)), ((), ())), preferred_element_type=jnp.float32
    )
    scaled = grad_normed * norm_gain
    grad_unit = (
        scaled
        - jnp.mean(scaled, axis=-1, keepdims=True)
        - unit_rows * jnp.mean(scaled * unit_rows, axis=-1, keepdims=True)
    )
    grad_packed = (grad_rows.astype(jnp.float32) + inv_dev * grad_unit).astype(jnp.bfloat16)
    back_slots = (
        jnp.zeros((groups * slot_count, features), jnp.bfloat16).at[pick_rows].set(grad_packed)
    )
    back_slots = back_slots.reshape(groups, slot_count, features)
    returned = lax.all_to_all(back_slots, "dp", split_axis=0, concat_axis=0, tiled=True).reshape(
        groups * slot_count, features
    )
    patch_grad = jnp.take(returned, row_slot, axis=0, mode="fill", fill_value=0)
    return (layer_out[None], patch_grad[None])


def solution(mesh):
    return jax.shard_map(
        local,
        mesh=mesh,
        in_specs=(
            P("dp", "tensor", None),
            P("dp", "tensor", None, None),
            P("dp", "tensor"),
            P("dp", "tensor"),
            P(),
            P("tensor", None),
            P("tensor", None),
            P("dp", "tensor", None),
        ),
        out_specs=(P("dp", "tensor", None), P("dp", "tensor", None)),
        check_vma=False,
    )
```

```python
import jax
import jax.numpy as jnp
from jax import lax
from jax.sharding import PartitionSpec as P

HD = 112
HEADS = 8
MOST = 96


def extended(block, sides, width):
    for axis, dim in sides:
        count = lax.axis_size(axis)
        forward = [(i, i + 1) for i in range(count - 1)]
        backward = [(target, source) for source, target in forward]
        low = lax.ppermute(
            lax.slice_in_dim(block, block.shape[dim] - width, None, axis=dim), axis, forward
        )
        high = lax.ppermute(lax.slice_in_dim(block, 0, width, axis=dim), axis, backward)
        block = jnp.concatenate([low, block, high], axis=dim)
    return block


def gather_weights(qkv_weight, out_weight):
    qkv_rows, qkv_cols = qkv_weight.shape
    out_rows, out_cols = out_weight.shape
    out_wide = out_weight.reshape(qkv_rows, out_rows * out_cols // qkv_rows)
    both = lax.all_gather(
        jnp.concatenate([qkv_weight, out_wide], axis=1), "tensor", axis=0, tiled=True
    )
    full_qkv = both[:, :qkv_cols]
    out_pairs = both[:, qkv_cols:]
    return full_qkv, out_pairs


def spread(cols, side):
    rows = cols.shape[0]
    none = jnp.zeros_like(cols)
    pair = (cols, none) if side == 0 else (none, cols)
    return jnp.stack(pair, axis=-1).reshape(rows, 2 * cols.shape[1])


def times_out(attended, out_pairs):
    halves = [
        jnp.dot(spread(attended, side), out_pairs, preferred_element_type=jnp.float32)
        for side in range(2)
    ]
    return jnp.concatenate(halves, axis=1)


def times_out_t(grad_rows, out_pairs):
    half = out_pairs.shape[1]
    rows = grad_rows.shape[0]
    parts = [
        lax.dot_general(
            grad_rows[:, side * half : (side + 1) * half],
            out_pairs,
            (((1,), (1,)), ((), ())),
            preferred_element_type=jnp.float32,
        ).reshape(rows, -1, 2)[:, :, side]
        for side in range(2)
    ]
    return parts[0] + parts[1]


def normalize(rows_in, norm_gain):
    values = rows_in.astype(jnp.float32)
    center = values - jnp.mean(values, axis=-1, keepdims=True)
    inv_dev = lax.rsqrt(jnp.mean(center * center, axis=-1, keepdims=True) + 1e-06)
    unit_rows = center * inv_dev
    return (values, unit_rows, inv_dev, (unit_rows * norm_gain).astype(jnp.bfloat16))


def head_blocks(rows_in, count):
    tiled = jnp.tile(rows_in, (HEADS, 1))
    row_head = lax.broadcasted_iota(jnp.int32, tiled.shape, 0) // count
    col_head = lax.broadcasted_iota(jnp.int32, tiled.shape, 1) // HD
    return jnp.where(row_head == col_head, tiled, jnp.zeros_like(tiled))


def own_heads(stacked, count):
    row_head = lax.broadcasted_iota(jnp.int32, stacked.shape, 0) // count
    col_head = lax.broadcasted_iota(jnp.int32, stacked.shape, 1) // HD
    kept = jnp.where(row_head == col_head, stacked, jnp.zeros_like(stacked))
    return kept.reshape(HEADS, count, stacked.shape[1]).sum(axis=0)


def rows_dot(a, b):
    return lax.dot_general(a, b, (((1,), (1,)), ((), ())), preferred_element_type=jnp.float32)


def cols_dot(a, b):
    return lax.dot_general(a, b, (((0,), (0,)), ((), ())), preferred_element_type=jnp.float32)


def attend(queries, keyval, seg_query, seg_key):
    all_heads = HEADS * HD
    score_scale = HD ** (-0.5)
    count = queries.shape[0]
    query_blocks = head_blocks(queries, count)
    scores = rows_dot(query_blocks, keyval[:, :all_heads]) * score_scale
    same_chart = jnp.tile(seg_query[:, None] == seg_key[None, :], (HEADS, 1))
    scores = jnp.where(same_chart, scores, -jnp.inf)
    row_max = jnp.max(scores, axis=1, keepdims=True)
    exp_scores = jnp.exp(scores - row_max)
    row_sum = jnp.sum(exp_scores, axis=1, keepdims=True)
    attn_probs = exp_scores / row_sum
    prob_low = attn_probs.astype(jnp.bfloat16)
    mixed = jnp.dot(prob_low, keyval[:, all_heads:], preferred_element_type=jnp.float32)
    attended = own_heads(mixed, count)
    return (attn_probs, prob_low, attended.astype(jnp.bfloat16), query_blocks)


def local(patch_rows, send_rows, take_rows, segments, norm_gain, qkv_weight, out_weight, grad_out):
    groups = lax.axis_size("dp")
    src_count = patch_rows.shape[1]
    features = patch_rows.shape[2]
    slot_count = send_rows.shape[3]
    own_rows = take_rows.shape[1]
    all_heads = HEADS * HD
    score_scale = HD ** (-0.5)
    patches = patch_rows[0]
    send_flat = send_rows.reshape(groups * slot_count)
    outgoing = jnp.take(patches, send_flat, axis=0, mode="fill", fill_value=0).reshape(
        groups, slot_count, features
    )
    incoming = lax.all_to_all(outgoing, "dp", split_axis=0, concat_axis=0, tiled=True).reshape(
        groups * slot_count, features
    )
    pick_rows = take_rows[0]
    slot_total = groups * slot_count
    row_slot = jnp.full((src_count + 1,), slot_total, jnp.int32).at[send_flat].set(
        jnp.arange(slot_total, dtype=jnp.int32)
    )[:src_count]
    packed = jnp.take(incoming, pick_rows, axis=0)
    full_qkv, full_out = gather_weights(qkv_weight, out_weight)
    values, unit_rows, inv_dev, normed = normalize(packed, norm_gain)
    wide_normed = extended(normed, (("tensor", 0),), MOST)
    queries = jnp.dot(
        normed, full_qkv[:, :all_heads], preferred_element_type=jnp.float32
    ).astype(jnp.bfloat16)
    wide_kv = jnp.dot(
        wide_normed, full_qkv[:, all_heads:], preferred_element_type=jnp.float32
    ).astype(jnp.bfloat16)
    seg_plus = segments[0] + 1
    wide_seg = extended(seg_plus, (("tensor", 0),), MOST)
    attn_probs, prob_low, attended, query_blocks = attend(queries, wide_kv, seg_plus, wide_seg)
    layer_out = (values + times_out(attended, full_out)).astype(jnp.bfloat16)
    grad_rows = grad_out[0]
    grad_att = times_out_t(grad_rows, full_out).astype(jnp.bfloat16)
    grad_blocks = head_blocks(grad_att, own_rows)
    dprobs = rows_dot(grad_blocks, wide_kv[:, all_heads:])
    row_inner = jnp.sum(attn_probs * dprobs, axis=1, keepdims=True)
    dscore = (attn_probs * (dprobs - row_inner) * score_scale).astype(jnp.bfloat16)
    window_rows = wide_kv.shape[0]
    score_rows = dscore.reshape(HEADS, own_rows, window_rows).transpose(1, 0, 2)
    grad_query = jnp.dot(
        score_rows.reshape(own_rows, HEADS * window_rows),
        head_blocks(wide_kv[:, :all_heads], window_rows),
        preferred_element_type=jnp.float32,
    )
    grad_key = cols_dot(dscore, query_blocks)
    grad_value = cols_dot(prob_low, grad_blocks)
    grad_window = jnp.concatenate([grad_key, grad_value], axis=1)
    center = grad_window[MOST : MOST + own_rows]
    blocks = lax.axis_size("tensor")
    ahead = [(i, i + 1) for i in range(blocks - 1)]
    behind = [(target, source) for source, target in ahead]
    high_rim, low_rim = lax.optimization_barrier((grad_window[MOST + own_rows :], grad_window[:MOST]))
    from_prev = lax.ppermute(high_rim, "tensor", ahead)
    from_next = lax.ppermute(low_rim, "tensor", behind)
    center = center.at[:MOST].add(from_prev)
    center = center.at[own_rows - MOST :].add(from_next)
    grad_proj = jnp.concatenate([grad_query, center], axis=1).astype(jnp.bfloat16)
    grad_normed = lax.dot_general(
        grad_proj, full_qkv, (((1,), (1,)), ((), ())), preferred_element_type=jnp.float32
    )
    scaled = grad_normed * norm_gain
    grad_unit = (
        scaled
        - jnp.mean(scaled, axis=-1, keepdims=True)
        - unit_rows * jnp.mean(scaled * unit_rows, axis=-1, keepdims=True)
    )
    grad_packed = (grad_rows.astype(jnp.float32) + inv_dev * grad_unit).astype(jnp.bfloat16)
    back_slots = (
        jnp.zeros((groups * slot_count, features), jnp.bfloat16).at[pick_rows].set(grad_packed)
    )
    back_slots = back_slots.reshape(groups, slot_count, features)
    returned = lax.all_to_all(back_slots, "dp", split_axis=0, concat_axis=0, tiled=True).reshape(
        groups * slot_count, features
    )
    patch_grad = jnp.take(returned, row_slot, axis=0, mode="fill", fill_value=0)
    return (layer_out[None], patch_grad[None])


def solution(mesh):
    return jax.shard_map(
        local,
        mesh=mesh,
        in_specs=(
            P("dp", "tensor", None),
            P("dp", "tensor", None, None),
            P("dp", "tensor"),
            P("dp", "tensor"),
            P(),
            P("tensor", None),
            P("tensor", None),
            P("dp", "tensor", None),
        ),
        out_specs=(P("dp", "tensor", None), P("dp", "tensor", None)),
        check_vma=False,
    )
```

```python
import jax
import jax.numpy as jnp
from jax import lax
from jax.sharding import PartitionSpec as P

HD = 112
HEADS = 8
MOST = 96


def extended(block, sides, width):
    for axis, dim in sides:
        count = lax.axis_size(axis)
        forward = [(i, i + 1) for i in range(count - 1)]
        backward = [(target, source) for source, target in forward]
        low = lax.ppermute(
            lax.slice_in_dim(block, block.shape[dim] - width, None, axis=dim), axis, forward
        )
        high = lax.ppermute(lax.slice_in_dim(block, 0, width, axis=dim), axis, backward)
        block = jnp.concatenate([low, block, high], axis=dim)
    return block


def gather_weights(qkv_weight, out_weight):
    qkv_rows, qkv_cols = qkv_weight.shape
    out_rows, out_cols = out_weight.shape
    out_wide = out_weight.reshape(qkv_rows, out_rows * out_cols // qkv_rows)
    both = lax.all_gather(
        jnp.concatenate([qkv_weight, out_wide], axis=1), "tensor", axis=0, tiled=True
    )
    full_qkv = both[:, :qkv_cols]
    out_pairs = both[:, qkv_cols:]
    return full_qkv, out_pairs


def spread(cols, side):
    rows = cols.shape[0]
    none = jnp.zeros_like(cols)
    pair = (cols, none) if side == 0 else (none, cols)
    return jnp.stack(pair, axis=-1).reshape(rows, 2 * cols.shape[1])


def times_out(attended, out_pairs):
    halves = [
        jnp.dot(spread(attended, side), out_pairs, preferred_element_type=jnp.float32)
        for side in range(2)
    ]
    return jnp.concatenate(halves, axis=1)


def times_out_t(grad_rows, out_pairs):
    half = out_pairs.shape[1]
    rows = grad_rows.shape[0]
    parts = [
        lax.dot_general(
            grad_rows[:, side * half : (side + 1) * half],
            out_pairs,
            (((1,), (1,)), ((), ())),
            preferred_element_type=jnp.float32,
        ).reshape(rows, -1, 2)[:, :, side]
        for side in range(2)
    ]
    return parts[0] + parts[1]


def normalize(rows_in, norm_gain):
    values = rows_in.astype(jnp.float32)
    center = values - jnp.mean(values, axis=-1, keepdims=True)
    inv_dev = lax.rsqrt(jnp.mean(center * center, axis=-1, keepdims=True) + 1e-06)
    unit_rows = center * inv_dev
    return (values, unit_rows, inv_dev, (unit_rows * norm_gain).astype(jnp.bfloat16))


def head_blocks(rows_in, count):
    tiled = jnp.tile(rows_in, (HEADS, 1))
    row_head = lax.broadcasted_iota(jnp.int32, tiled.shape, 0) // count
    col_head = lax.broadcasted_iota(jnp.int32, tiled.shape, 1) // HD
    return jnp.where(row_head == col_head, tiled, jnp.zeros_like(tiled))


def own_heads(stacked, count):
    row_head = lax.broadcasted_iota(jnp.int32, stacked.shape, 0) // count
    col_head = lax.broadcasted_iota(jnp.int32, stacked.shape, 1) // HD
    kept = jnp.where(row_head == col_head, stacked, jnp.zeros_like(stacked))
    return kept.reshape(HEADS, count, stacked.shape[1]).sum(axis=0)


def rows_dot(a, b):
    return lax.dot_general(a, b, (((1,), (1,)), ((), ())), preferred_element_type=jnp.float32)


def cols_dot(a, b):
    return lax.dot_general(a, b, (((0,), (0,)), ((), ())), preferred_element_type=jnp.float32)


def attend(queries, keyval, seg_query, seg_key):
    all_heads = HEADS * HD
    score_scale = HD ** (-0.5)
    count = queries.shape[0]
    query_blocks = head_blocks(queries, count)
    scores = rows_dot(query_blocks, keyval[:, :all_heads]) * score_scale
    same_chart = jnp.tile(seg_query[:, None] == seg_key[None, :], (HEADS, 1))
    scores = jnp.where(same_chart, scores, -jnp.inf)
    row_max = jnp.max(scores, axis=1, keepdims=True)
    exp_scores = jnp.exp(scores - row_max)
    row_sum = jnp.sum(exp_scores, axis=1, keepdims=True)
    attn_probs = exp_scores / row_sum
    prob_low = attn_probs.astype(jnp.bfloat16)
    mixed = jnp.dot(prob_low, keyval[:, all_heads:], preferred_element_type=jnp.float32)
    attended = own_heads(mixed, count)
    return (attn_probs, prob_low, attended.astype(jnp.bfloat16), query_blocks)


def local(patch_rows, send_rows, take_rows, segments, norm_gain, qkv_weight, out_weight, grad_out):
    groups = lax.axis_size("dp")
    src_count = patch_rows.shape[1]
    features = patch_rows.shape[2]
    slot_count = send_rows.shape[3]
    own_rows = take_rows.shape[1]
    all_heads = HEADS * HD
    score_scale = HD ** (-0.5)
    patches = patch_rows[0]
    send_flat = send_rows.reshape(groups * slot_count)
    outgoing = jnp.take(patches, send_flat, axis=0, mode="fill", fill_value=0).reshape(
        groups, slot_count, features
    )
    incoming = lax.all_to_all(outgoing, "dp", split_axis=0, concat_axis=0, tiled=True).reshape(
        groups * slot_count, features
    )
    pick_rows = take_rows[0]
    slot_total = groups * slot_count
    row_slot = jnp.full((src_count + 1,), slot_total, jnp.int32).at[send_flat].set(
        jnp.arange(slot_total, dtype=jnp.int32)
    )[:src_count]
    packed = jnp.take(incoming, pick_rows, axis=0)
    full_qkv, full_out = gather_weights(qkv_weight, out_weight)
    values, unit_rows, inv_dev, normed = normalize(packed, norm_gain)
    projected = jnp.dot(normed, full_qkv, preferred_element_type=jnp.float32).astype(jnp.bfloat16)
    queries = projected[:, :all_heads]
    keyval = projected[:, all_heads:]
    seg_plus = segments[0] + 1
    wide_kv, wide_seg = (
        extended(keyval, (("tensor", 0),), MOST),
        extended(seg_plus, (("tensor", 0),), MOST),
    )
    attn_probs, prob_low, attended, query_blocks = attend(queries, wide_kv, seg_plus, wide_seg)
    layer_out = (values + times_out(attended, full_out)).astype(jnp.bfloat16)
    grad_rows = grad_out[0]
    grad_att = times_out_t(grad_rows, full_out).astype(jnp.bfloat16)
    grad_blocks = head_blocks(grad_att, own_rows)
    dprobs = rows_dot(grad_blocks, wide_kv[:, all_heads:])
    row_inner = jnp.sum(attn_probs * dprobs, axis=1, keepdims=True)
    dscore = (attn_probs * (dprobs - row_inner) * score_scale).astype(jnp.bfloat16)
    window_rows = wide_kv.shape[0]
    score_rows = dscore.reshape(HEADS, own_rows, window_rows).transpose(1, 0, 2)
    grad_query = jnp.dot(
        score_rows.reshape(own_rows, HEADS * window_rows),
        head_blocks(wide_kv[:, :all_heads], window_rows),
        preferred_element_type=jnp.float32,
    )
    grad_key = cols_dot(dscore, query_blocks)
    grad_value = cols_dot(prob_low, grad_blocks)
    grad_window = jnp.concatenate([grad_key, grad_value], axis=1)
    center = grad_window[MOST : MOST + own_rows]
    blocks = lax.axis_size("tensor")
    ahead = [(i, i + 1) for i in range(blocks - 1)]
    behind = [(target, source) for source, target in ahead]
    high_rim, low_rim = lax.optimization_barrier((grad_window[MOST + own_rows :], grad_window[:MOST]))
    from_prev = lax.ppermute(high_rim, "tensor", ahead)
    from_next = lax.ppermute(low_rim, "tensor", behind)
    center = center.at[:MOST].add(from_prev)
    center = center.at[own_rows - MOST :].add(from_next)
    grad_proj = jnp.concatenate([grad_query, center], axis=1).astype(jnp.bfloat16)
    grad_normed = lax.dot_general(
        grad_proj, full_qkv, (((1,), (1,)), ((), ())), preferred_element_type=jnp.float32
    )
    scaled = grad_normed * norm_gain
    grad_unit = (
        scaled
        - jnp.mean(scaled, axis=-1, keepdims=True)
        - unit_rows * jnp.mean(scaled * unit_rows, axis=-1, keepdims=True)
    )
    grad_packed = (grad_rows.astype(jnp.float32) + inv_dev * grad_unit).astype(jnp.bfloat16)
    back_slots = (
        jnp.zeros((groups * slot_count, features), jnp.bfloat16).at[pick_rows].set(grad_packed)
    )
    returned = lax.all_to_all(back_slots, "dp", split_axis=0, concat_axis=0, tiled=True)
    patch_grad = jnp.take(returned, row_slot, axis=0, mode="fill", fill_value=0)
    return (layer_out[None], patch_grad[None])


def solution(mesh):
    return jax.shard_map(
        local,
        mesh=mesh,
        in_specs=(
            P("dp", "tensor", None),
            P("dp", "tensor", None, None),
            P("dp", "tensor"),
            P("dp", "tensor"),
            P(),
            P("tensor", None),
            P("tensor", None),
            P("dp", "tensor", None),
        ),
        out_specs=(P("dp", "tensor", None), P("dp", "tensor", None)),
        check_vma=False,
    )
```

```python
import jax
import jax.numpy as jnp
from jax import lax
from jax.sharding import PartitionSpec as P

HD = 112
HEADS = 8
MOST = 96


def extended(block, sides, width):
    for axis, dim in sides:
        count = lax.axis_size(axis)
        forward = [(i, i + 1) for i in range(count - 1)]
        backward = [(target, source) for source, target in forward]
        low = lax.ppermute(
            lax.slice_in_dim(block, block.shape[dim] - width, None, axis=dim), axis, forward
        )
        high = lax.ppermute(lax.slice_in_dim(block, 0, width, axis=dim), axis, backward)
        block = jnp.concatenate([low, block, high], axis=dim)
    return block


def gather_weights(qkv_weight, out_weight):
    qkv_rows, qkv_cols = qkv_weight.shape
    out_rows, out_cols = out_weight.shape
    out_wide = out_weight.reshape(qkv_rows, out_rows * out_cols // qkv_rows)
    both = lax.all_gather(
        jnp.concatenate([qkv_weight, out_wide], axis=1), "tensor", axis=0, tiled=True
    )
    full_qkv = both[:, :qkv_cols]
    out_pairs = both[:, qkv_cols:]
    return full_qkv, out_pairs


def spread(cols, side):
    rows = cols.shape[0]
    none = jnp.zeros_like(cols)
    pair = (cols, none) if side == 0 else (none, cols)
    return jnp.stack(pair, axis=-1).reshape(rows, 2 * cols.shape[1])


def times_out(attended, out_pairs):
    halves = [
        jnp.dot(spread(attended, side), out_pairs, preferred_element_type=jnp.float32)
        for side in range(2)
    ]
    return jnp.concatenate(halves, axis=1)


def times_out_t(grad_rows, out_pairs):
    half = out_pairs.shape[1]
    rows = grad_rows.shape[0]
    parts = [
        lax.dot_general(
            grad_rows[:, side * half : (side + 1) * half],
            out_pairs,
            (((1,), (1,)), ((), ())),
            preferred_element_type=jnp.float32,
        )
        for side in range(2)
    ]
    even = lax.broadcasted_iota(jnp.int32, parts[0].shape, 1) % 2 == 0
    return jnp.where(even, parts[0], parts[1]).reshape(rows, -1, 2).sum(axis=2)


def normalize(rows_in, norm_gain):
    values = rows_in.astype(jnp.float32)
    center = values - jnp.mean(values, axis=-1, keepdims=True)
    inv_dev = lax.rsqrt(jnp.mean(center * center, axis=-1, keepdims=True) + 1e-06)
    unit_rows = center * inv_dev
    return (values, unit_rows, inv_dev, (unit_rows * norm_gain).astype(jnp.bfloat16))


def head_blocks(rows_in, count):
    tiled = jnp.tile(rows_in, (HEADS, 1))
    row_head = lax.broadcasted_iota(jnp.int32, tiled.shape, 0) // count
    col_head = lax.broadcasted_iota(jnp.int32, tiled.shape, 1) // HD
    return jnp.where(row_head == col_head, tiled, jnp.zeros_like(tiled))


def own_heads(stacked, count):
    row_head = lax.broadcasted_iota(jnp.int32, stacked.shape, 0) // count
    col_head = lax.broadcasted_iota(jnp.int32, stacked.shape, 1) // HD
    kept = jnp.where(row_head == col_head, stacked, jnp.zeros_like(stacked))
    return kept.reshape(HEADS, count, stacked.shape[1]).sum(axis=0)


def rows_dot(a, b):
    return lax.dot_general(a, b, (((1,), (1,)), ((), ())), preferred_element_type=jnp.float32)


def cols_dot(a, b):
    return lax.dot_general(a, b, (((0,), (0,)), ((), ())), preferred_element_type=jnp.float32)


def attend(queries, keyval, seg_query, seg_key):
    all_heads = HEADS * HD
    score_scale = HD ** (-0.5)
    count = queries.shape[0]
    query_blocks = head_blocks(queries, count)
    scores = rows_dot(query_blocks, keyval[:, :all_heads]) * score_scale
    same_chart = jnp.tile(seg_query[:, None] == seg_key[None, :], (HEADS, 1))
    scores = jnp.where(same_chart, scores, -jnp.inf)
    row_max = jnp.max(scores, axis=1, keepdims=True)
    exp_scores = jnp.exp(scores - row_max)
    row_sum = jnp.sum(exp_scores, axis=1, keepdims=True)
    attn_probs = exp_scores / row_sum
    prob_low = attn_probs.astype(jnp.bfloat16)
    mixed = jnp.dot(prob_low, keyval[:, all_heads:], preferred_element_type=jnp.float32)
    attended = own_heads(mixed, count)
    return (attn_probs, prob_low, attended.astype(jnp.bfloat16), query_blocks)


def local(patch_rows, send_rows, take_rows, segments, norm_gain, qkv_weight, out_weight, grad_out):
    groups = lax.axis_size("dp")
    src_count = patch_rows.shape[1]
    features = patch_rows.shape[2]
    slot_count = send_rows.shape[3]
    own_rows = take_rows.shape[1]
    all_heads = HEADS * HD
    score_scale = HD ** (-0.5)
    patches = patch_rows[0]
    send_flat = send_rows.reshape(groups * slot_count)
    outgoing = jnp.take(patches, send_flat, axis=0, mode="fill", fill_value=0).reshape(
        groups, slot_count, features
    )
    incoming = lax.all_to_all(outgoing, "dp", split_axis=0, concat_axis=0, tiled=True).reshape(
        groups * slot_count, features
    )
    pick_rows = take_rows[0]
    slot_total = groups * slot_count
    row_slot = jnp.full((src_count + 1,), slot_total, jnp.int32).at[send_flat].set(
        jnp.arange(slot_total, dtype=jnp.int32)
    )[:src_count]
    packed = jnp.take(incoming, pick_rows, axis=0)
    full_qkv, full_out = gather_weights(qkv_weight, out_weight)
    values, unit_rows, inv_dev, normed = normalize(packed, norm_gain)
    projected = jnp.dot(normed, full_qkv, preferred_element_type=jnp.float32).astype(jnp.bfloat16)
    queries = projected[:, :all_heads]
    keyval = projected[:, all_heads:]
    seg_plus = segments[0] + 1
    wide_kv, wide_seg = (
        extended(keyval, (("tensor", 0),), MOST),
        extended(seg_plus, (("tensor", 0),), MOST),
    )
    attn_probs, prob_low, attended, query_blocks = attend(queries, wide_kv, seg_plus, wide_seg)
    layer_out = (values + times_out(attended, full_out)).astype(jnp.bfloat16)
    grad_rows = grad_out[0]
    grad_att = times_out_t(grad_rows, full_out).astype(jnp.bfloat16)
    grad_blocks = head_blocks(grad_att, own_rows)
    dprobs = rows_dot(grad_blocks, wide_kv[:, all_heads:])
    row_inner = jnp.sum(attn_probs * dprobs, axis=1, keepdims=True)
    dscore = (attn_probs * (dprobs - row_inner) * score_scale).astype(jnp.bfloat16)
    window_rows = wide_kv.shape[0]
    score_rows = dscore.reshape(HEADS, own_rows, window_rows).transpose(1, 0, 2)
    grad_query = jnp.dot(
        score_rows.reshape(own_rows, HEADS * window_rows),
        head_blocks(wide_kv[:, :all_heads], window_rows),
        preferred_element_type=jnp.float32,
    )
    grad_key = cols_dot(dscore, query_blocks)
    grad_value = cols_dot(prob_low, grad_blocks)
    grad_window = jnp.concatenate([grad_key, grad_value], axis=1)
    center = grad_window[MOST : MOST + own_rows]
    blocks = lax.axis_size("tensor")
    ahead = [(i, i + 1) for i in range(blocks - 1)]
    behind = [(target, source) for source, target in ahead]
    high_rim, low_rim = lax.optimization_barrier((grad_window[MOST + own_rows :], grad_window[:MOST]))
    from_prev = lax.ppermute(high_rim, "tensor", ahead)
    from_next = lax.ppermute(low_rim, "tensor", behind)
    center = center.at[:MOST].add(from_prev)
    center = center.at[own_rows - MOST :].add(from_next)
    grad_proj = jnp.concatenate([grad_query, center], axis=1).astype(jnp.bfloat16)
    grad_normed = lax.dot_general(
        grad_proj, full_qkv, (((1,), (1,)), ((), ())), preferred_element_type=jnp.float32
    )
    scaled = grad_normed * norm_gain
    grad_unit = (
        scaled
        - jnp.mean(scaled, axis=-1, keepdims=True)
        - unit_rows * jnp.mean(scaled * unit_rows, axis=-1, keepdims=True)
    )
    grad_packed = (grad_rows.astype(jnp.float32) + inv_dev * grad_unit).astype(jnp.bfloat16)
    back_slots = (
        jnp.zeros((groups * slot_count, features), jnp.bfloat16).at[pick_rows].set(grad_packed)
    )
    back_slots = back_slots.reshape(groups, slot_count, features)
    returned = lax.all_to_all(back_slots, "dp", split_axis=0, concat_axis=0, tiled=True).reshape(
        groups * slot_count, features
    )
    patch_grad = jnp.take(returned, row_slot, axis=0, mode="fill", fill_value=0)
    return (layer_out[None], patch_grad[None])


def solution(mesh):
    return jax.shard_map(
        local,
        mesh=mesh,
        in_specs=(
            P("dp", "tensor", None),
            P("dp", "tensor", None, None),
            P("dp", "tensor"),
            P("dp", "tensor"),
            P(),
            P("tensor", None),
            P("tensor", None),
            P("dp", "tensor", None),
        ),
        out_specs=(P("dp", "tensor", None), P("dp", "tensor", None)),
        check_vma=False,
    )
```
